512 devices in a mesh: dp: 64 (over z, y_lo, core), expert: 8 (over y_hi, x).
Axes of the slice: x: 4, y: 4 (y_hi: 2, y_lo: 2; y = y_hi * 2 + y_lo), z: 16, core: 2. Of those that a mesh axis runs over, the one named last changes fastest.
Arguments:
- inputs: bfloat16 [256, 3072], P('dp', 'expert'), may hold values from -6 to 6
- routes: int32 [256, 2], P('dp'), may hold values from 0 to 7, all different within a row; in each aligned block of 4 rows (0 to 3, 4 to 7, ...) at most 2 rows name the same one
- combine: float32 [256, 2], P('dp'), may hold values from 0.1 to 1
- cotangent: bfloat16 [256, 3072], P('dp', 'expert'), may hold values from -6 to 6
- w_gate: bfloat16 [8, 3072, 8192], P('expert', None, 'dp'), may hold values from -0.109375 to 0.109375
- w_up: bfloat16 [8, 3072, 8192], P('expert', None, 'dp'), may hold values from -0.109375 to 0.109375
- w_down: bfloat16 [8, 8192, 3072], P('expert', 'dp'), may hold values from -0.0625 to 0.0625
Outputs:
- input_grad: bfloat16 [256, 3072], P('dp', 'expert')
- gate_grad: bfloat16 [8, 3072, 8192], P('expert', None, 'dp')
- up_grad: bfloat16 [8, 3072, 8192], P('expert', None, 'dp')
- down_grad: bfloat16 [8, 8192, 3072], P('expert', 'dp')
The draws below stay inside these ranges and needn't reach their ends.
Inputs may be any that keep to these rules, and one draw needn't show every extreme that they name: `routes`: each token names two different experts. Among the tokens of one index of dp no expert is named more than 2 times, a bound that some block reaches there.
All inputs are finite; a program needn't handle non-finite values.
Results may differ from the reference program's by a relative error of at most 0.0065.
Values may be sent and summed in bfloat16 or wider, within the bound.
No kernel may reach another device: no remote copies, remote signals or barrier semaphores. Data moves between devices by JAX's collectives and lax.ppermute only.
A program may use at most 64 MiB of HBM per device.

```python
import math
import jax
import jax.numpy as jnp
import numpy as np
from jax import lax

D = 3072
FF = 8192
EXPERTS = 8
MOST = 2
TOK_DP = 4
TOKENS = 256
N_DP = 64


def steps_of(stream_key, extent, cuts, least, largest):
    loudness, own = 1.0, jax.random.fold_in(stream_key, 6)
    for axis_at, blocks in cuts:
        draws = jnp.exp(jax.random.uniform(jax.random.fold_in(own, axis_at), (blocks,), jnp.float32, least / len(cuts), largest / len(cuts)))
        loudness = loudness * jnp.repeat(draws, extent[axis_at] // blocks).reshape([-1 if axis == axis_at else 1 for axis in range(len(extent))])
    return loudness


def routed_block(key, own, number, rows, count, top, most, skew):
    ranking = jax.random.permutation(key, count)
    crowded, usual = load_shares(count, rows * top, most, skew, True), load_shares(count, rows * top, most, skew, False)
    places = jnp.arange(count)

    def named(tallies, turn):
        used = int((tallies > 0).sum())
        fixed = max(1, used // 4)
        passed = fixed + (places - fixed + turn * (used - fixed)) % max(1, count - fixed)
        return jnp.zeros((count,), jnp.int32).at[ranking[jnp.where(places < fixed, places, passed)]].set(jnp.asarray(tallies, jnp.int32))

    tallies = jnp.where(number % 4 == 0, named(crowded, number // 4), named(usual, number - number // 4 - 1))
    mixed = jax.random.permutation(jax.random.fold_in(own, 3), count)
    giver, sink = mixed[0:count // 2 * 2:2], mixed[1:count // 2 * 2:2]
    slack = jnp.minimum(tallies[giver] - 1, most - tallies[sink]) // 2
    slack = jnp.where((giver == ranking[0]) | (sink == ranking[0]) | (tallies[sink] == 0), 0, jnp.maximum(slack, 0))
    passed = jax.random.randint(jax.random.fold_in(own, 4), (count // 2,), 0, 1 << 20) % (slack + 1)
    tallies = tallies.at[giver].add(-passed).at[sink].add(passed)
    labels = jnp.searchsorted(jnp.cumsum(tallies), jnp.arange(rows * top), side="right").astype(jnp.int32)
    table = labels.reshape(top, rows).T
    table = table[jax.random.permutation(jax.random.fold_in(own, 1), rows)]
    turn = jax.random.randint(jax.random.fold_in(own, 2), (rows, 1), 0, top)
    return jnp.take_along_axis(table, (jnp.arange(top)[None, :] + turn) % top, axis=1)


def load_shares(number_of, total, bound, slope, full):
    portions = [(1 << 20) // math.isqrt(grade ** slope) + 1 for grade in range(1, number_of + 1)]
    largest = bound if full else min(bound, max(-(-total // number_of), total * portions[0] // sum(portions)))
    least = 1 if total - largest >= number_of - 1 else 0
    counts, surplus = [largest] + [least] * (number_of - 1), total - largest - least * (number_of - 1)
    while surplus > 0:
        candidates = [i for i in range(1, number_of) if counts[i] < largest] or [i for i in range(1, number_of) if counts[i] < bound]
        pool, remaining = sum([portions[i] for i in candidates]), surplus
        for i in candidates:
            more = min(bound - counts[i], max(1, remaining * portions[i] // pool), surplus)
            counts[i] = counts[i] + more
            surplus = surplus - more
    return np.array(counts)


def scatter_about(key, extent, scale, reach, cuts=(), kind=jnp.bfloat16):
    values = jax.random.normal(key, extent, jnp.float32) * scale
    if len(cuts) > 0:
        values = steps_of(key, extent, cuts, -0.22, 0.18) * values
    return jnp.clip(values, min=-reach, max=reach).astype(kind)


def setup_inputs(seed: int = 0) -> dict:
    keys = jax.random.split(jax.random.key(seed), 8)
    inputs = scatter_about(keys[0], (TOKENS, D), 1.0, 6.0, ((0, 64), (1, 8)))
    routes_keys = jax.random.split(jax.random.fold_in(keys[1], 1), TOKENS // TOK_DP)
    routes_turns = jax.random.permutation(jax.random.fold_in(keys[1], 3), TOKENS // TOK_DP)
    routes = jax.vmap(lambda own, number: routed_block(jax.random.fold_in(keys[1], 2), own, number, TOK_DP, EXPERTS, 2, MOST, 2))(routes_keys, routes_turns).reshape((TOKENS, 2))
    combine = jnp.clip(0.1 + 0.9 * jax.random.uniform(keys[2], (TOKENS, 2), jnp.float32) ** steps_of(keys[2], (TOKENS, 2), ((0, 64),), -0.2, 0.2), 0.1, 1.0)
    cotangent = scatter_about(keys[3], (TOKENS, D), 1.0, 6.0, ((0, 64), (1, 8)))
    w_gate = scatter_about(keys[4], (EXPERTS, D, FF), D ** -0.5, 0.109375, ((0, 8), (2, 64)))
    w_up = scatter_about(keys[5], (EXPERTS, D, FF), D ** -0.5, 0.109375, ((0, 8), (2, 64)))
    w_down = scatter_about(keys[6], (EXPERTS, FF, D), FF ** -0.5, 0.0625, ((0, 8), (1, 64)))
    return dict(inputs=inputs, routes=routes, combine=combine, cotangent=cotangent, w_gate=w_gate, w_up=w_up, w_down=w_down)


def reference(inputs, routes, combine, cotangent, w_gate, w_up, w_down):
    capacity = N_DP * MOST
    routes_flat = routes.reshape(-1)
    repeated = jnp.repeat(inputs, 2, axis=0)
    scaled = (combine.reshape(-1)[:, None] * jnp.repeat(cotangent, 2, axis=0).astype(jnp.float32)).astype(jnp.bfloat16)

    def per_expert(packed):
        expert_id, gate_w, up_w, down_w = packed
        member = (routes_flat == expert_id).astype(jnp.int32)
        rank_index = jnp.cumsum(member) - member
        hit = (rank_index[:, None] == jnp.arange(capacity, dtype=jnp.int32)[None, :]) & (member[:, None] == 1)
        selector = hit.astype(jnp.float32)
        chooser = selector.T.astype(jnp.bfloat16)
        rows_in = jnp.dot(chooser, repeated, preferred_element_type=jnp.float32).astype(jnp.bfloat16)
        rows_grad = jnp.dot(chooser, scaled, preferred_element_type=jnp.float32).astype(jnp.bfloat16)
        gate_pre = jnp.dot(rows_in, gate_w, preferred_element_type=jnp.float32)
        up_pre = jnp.dot(rows_in, up_w, preferred_element_type=jnp.float32)
        gate_sig = jax.nn.sigmoid(gate_pre)
        activated = gate_pre * gate_sig
        hidden = (activated * up_pre).astype(jnp.bfloat16)
        hidden_delta = jnp.dot(rows_grad, down_w.T, preferred_element_type=jnp.float32)
        down_grad = jnp.dot(hidden.T, rows_grad, preferred_element_type=jnp.float32).astype(jnp.bfloat16)
        gate_delta = (hidden_delta * up_pre * gate_sig * (1.0 + gate_pre * (1.0 - gate_sig))).astype(jnp.bfloat16)
        up_delta = (hidden_delta * activated).astype(jnp.bfloat16)
        gate_grad = jnp.dot(rows_in.T, gate_delta, preferred_element_type=jnp.float32).astype(jnp.bfloat16)
        up_grad = jnp.dot(rows_in.T, up_delta, preferred_element_type=jnp.float32).astype(jnp.bfloat16)
        row_grads = jnp.dot(gate_delta, gate_w.T, preferred_element_type=jnp.float32) + jnp.dot(up_delta, up_w.T, preferred_element_type=jnp.float32)
        contribution = jnp.dot(selector, row_grads, precision=lax.Precision.HIGHEST)
        return contribution, gate_grad, up_grad, down_grad

    contributions, gate_grad, up_grad, down_grad = lax.map(per_expert, (jnp.arange(EXPERTS, dtype=jnp.int32), w_gate, w_up, w_down))
    assign_grad = jnp.sum(contributions, axis=0)
    input_grad = jnp.sum(assign_grad.reshape(TOKENS, 2, D), axis=1).astype(jnp.bfloat16)
    return (input_grad, gate_grad, up_grad, down_grad)
```

```python
import jax
import jax.numpy as jnp
from jax import lax
from jax.sharding import Mesh, PartitionSpec as P

MOST = 2
DP = ("z", "y_lo", "core")
EX = ("y_hi", "x")


def forward_part(rows_in, w_gate, w_up):
    gate_pre = jnp.dot(rows_in, w_gate, preferred_element_type=jnp.float32)
    up_pre = jnp.dot(rows_in, w_up, preferred_element_type=jnp.float32)
    gate_sig = jax.nn.sigmoid(gate_pre)
    activated = gate_pre * gate_sig
    hidden = (activated * up_pre).astype(jnp.bfloat16)
    return (gate_pre, up_pre, gate_sig, activated, hidden)


def gather_dp(block):
    block = lax.all_gather(block, "core", axis=0)
    block = lax.all_gather(block, "y_lo", axis=0)
    block = lax.all_gather(block, "z", axis=0)
    return block.reshape((-1,) + block.shape[3:])


def per_device(inputs, routes, combine, cotangent, w_gate, w_up, w_down):
    tok = inputs.shape[0]
    width_part = inputs.shape[1]
    n_ex = lax.axis_size(EX)
    n_dp = lax.axis_size(DP)
    capacity = n_dp * MOST
    slots_in_block = 2 * tok

    scaled = (
        combine.reshape(-1)[:, None] * jnp.repeat(cotangent, 2, axis=0).astype(jnp.float32)
    ).astype(jnp.bfloat16)
    route_row = jnp.zeros((1, width_part), jnp.bfloat16)
    route_row = route_row.at[0, :slots_in_block].set(routes.reshape(-1).astype(jnp.bfloat16))
    packed = jnp.concatenate([inputs, scaled, route_row], axis=0)
    pad_rows = (-packed.shape[0]) % 16
    packed = jnp.pad(packed, ((0, pad_rows), (0, 0)))
    every = gather_dp(packed)
    all_in = every[:, :tok, :].reshape(n_dp * tok, width_part)
    all_scaled = every[:, tok : 3 * tok, :].reshape(n_dp * slots_in_block, width_part)
    all_routes = every[:, 3 * tok, :slots_in_block].astype(jnp.int32)

    onehot = (all_routes[:, :, None] == jnp.arange(n_ex, dtype=jnp.int32)).astype(jnp.int32)
    before = jnp.cumsum(onehot, axis=1) - onehot
    rank = jnp.sum(before * onehot, axis=2)
    block_id = jnp.arange(n_dp, dtype=jnp.int32)[:, None]
    column = (all_routes * capacity + block_id * MOST + rank).reshape(-1)
    placer = column[:, None] == jnp.arange(n_ex * capacity, dtype=jnp.int32)[None, :]
    placer_tok = jnp.any(placer.reshape(n_dp * tok, 2, n_ex * capacity), axis=1)

    sent_in = jnp.dot(
        placer_tok.astype(jnp.bfloat16).T, all_in, preferred_element_type=jnp.float32
    ).astype(jnp.bfloat16)
    sent_grad = jnp.dot(
        placer.astype(jnp.bfloat16).T, all_scaled, preferred_element_type=jnp.float32
    ).astype(jnp.bfloat16)
    sent = jnp.concatenate([sent_in, sent_grad], axis=1).reshape(n_ex, capacity, 2 * width_part)
    got = lax.all_to_all(sent, EX, 0, 0, tiled=True)
    got = got.reshape(n_ex, capacity, 2, width_part).transpose(2, 1, 0, 3)
    rows_in = got[0].reshape(capacity, n_ex * width_part)
    rows_grad = got[1].reshape(capacity, n_ex * width_part)

    gate_w, up_w, down_w = w_gate[0], w_up[0], w_down[0]
    gate_pre, up_pre, gate_sig, activated, hidden = forward_part(rows_in, gate_w, up_w)
    hidden_delta = jnp.dot(rows_grad, down_w.T, preferred_element_type=jnp.float32)
    down_grad = jnp.dot(hidden.T, rows_grad, preferred_element_type=jnp.float32).astype(
        jnp.bfloat16
    )
    gate_delta = (hidden_delta * up_pre * gate_sig * (1.0 + gate_pre * (1.0 - gate_sig))).astype(
        jnp.bfloat16
    )
    up_delta = (hidden_delta * activated).astype(jnp.bfloat16)
    gate_grad = jnp.dot(rows_in.T, gate_delta, preferred_element_type=jnp.float32).astype(
        jnp.bfloat16
    )
    up_grad = jnp.dot(rows_in.T, up_delta, preferred_element_type=jnp.float32).astype(jnp.bfloat16)
    from_gate = jnp.dot(gate_delta, gate_w.T, preferred_element_type=jnp.float32)
    from_up = jnp.dot(up_delta, up_w.T, preferred_element_type=jnp.float32)
    partial = (from_gate + from_up).reshape(capacity, n_ex, width_part).transpose(1, 0, 2)
    back = lax.all_to_all(partial, EX, 0, 0, tiled=True).reshape(n_ex * capacity, width_part)
    token_part = jnp.dot(
        placer_tok.astype(jnp.float32), back, precision=lax.Precision.HIGHEST
    )
    owned = lax.all_to_all(token_part.reshape(n_dp, tok, width_part), DP, 0, 0, tiled=True)
    input_grad = jnp.sum(owned, axis=0).astype(jnp.bfloat16)
    return (input_grad, gate_grad[None], up_grad[None], down_grad[None])


def solution(mesh):
    n_dp, n_ex = mesh.shape["dp"], mesh.shape["expert"]
    fine = Mesh(mesh.devices.reshape(n_dp // 4, 2, 2, 2, n_ex // 2), DP + EX)
    placed = (
        P(DP, EX),
        P(DP, None),
        P(DP, None),
        P(DP, EX),
        P(EX, None, DP),
        P(EX, None, DP),
        P(EX, DP, None),
    )
    return jax.shard_map(
        per_device,
        mesh=fine,
        in_specs=placed,
        out_specs=(
            P(DP, EX),
            P(EX, None, DP),
            P(EX, None, DP),
            P(EX, DP, None),
        ),
        check_vma=False,
    )
```

```python
import jax
import jax.numpy as jnp
from jax import lax
from jax.sharding import Mesh, PartitionSpec as P

MOST = 2
DP = ("z", "y_lo", "core")
EX = ("y_hi", "x")
CLASS = ("y_lo", "core")
LOCAL = CLASS + EX


def forward_part(rows_in, w_gate, w_up):
    gate_pre = jnp.dot(rows_in, w_gate, preferred_element_type=jnp.float32)
    up_pre = jnp.dot(rows_in, w_up, preferred_element_type=jnp.float32)
    gate_sig = jax.nn.sigmoid(gate_pre)
    activated = gate_pre * gate_sig
    hidden = (activated * up_pre).astype(jnp.bfloat16)
    return (gate_pre, up_pre, gate_sig, activated, hidden)


def per_device(inputs, routes, combine, cotangent, w_gate, w_up, w_down):
    tok = inputs.shape[0]
    width_part = inputs.shape[1]
    n_ex = lax.axis_size(EX)
    n_z = lax.axis_size("z")
    n_class = lax.axis_size(CLASS)
    per_class = n_z * MOST
    capacity = n_class * per_class
    slots_in_block = 2 * tok

    scaled = (
        combine.reshape(-1)[:, None] * jnp.repeat(cotangent, 2, axis=0).astype(jnp.float32)
    ).astype(jnp.bfloat16)
    route_row = jnp.zeros((1, width_part), jnp.bfloat16)
    route_row = route_row.at[0, :slots_in_block].set(routes.reshape(-1).astype(jnp.bfloat16))
    packed = jnp.concatenate([inputs, scaled, route_row], axis=0)
    pad_rows = (-packed.shape[0]) % 16
    packed = jnp.pad(packed, ((0, pad_rows), (0, 0)))
    every = lax.all_gather(packed, "z", axis=0)
    class_in = every[:, :tok, :].reshape(n_z * tok, width_part)
    class_scaled = every[:, tok : 3 * tok, :].reshape(n_z * slots_in_block, width_part)
    class_routes = every[:, 3 * tok, :slots_in_block].astype(jnp.int32)

    onehot = (class_routes[:, :, None] == jnp.arange(n_ex, dtype=jnp.int32)).astype(jnp.int32)
    before = jnp.cumsum(onehot, axis=1) - onehot
    rank = jnp.sum(before * onehot, axis=2)
    block_id = jnp.arange(n_z, dtype=jnp.int32)[:, None]
    column = (class_routes * per_class + block_id * MOST + rank).reshape(-1)
    placer = column[:, None] == jnp.arange(n_ex * per_class, dtype=jnp.int32)[None, :]
    placer_tok = jnp.any(placer.reshape(n_z * tok, 2, n_ex * per_class), axis=1)

    sent_in = jnp.dot(
        placer_tok.astype(jnp.bfloat16).T, class_in, preferred_element_type=jnp.float32
    ).astype(jnp.bfloat16)
    sent_grad = jnp.dot(
        placer.astype(jnp.bfloat16).T, class_scaled, preferred_element_type=jnp.float32
    ).astype(jnp.bfloat16)
    sent = jnp.concatenate([sent_in, sent_grad], axis=1).reshape(n_ex, per_class, 2 * width_part)
    sent = jnp.broadcast_to(sent[None], (n_class,) + sent.shape)
    sent = sent.reshape(n_class * n_ex, per_class, 2 * width_part)
    got = lax.all_to_all(sent, LOCAL, 0, 0, tiled=True)
    got = got.reshape(n_class, n_ex, per_class, 2, width_part).transpose(3, 0, 2, 1, 4)
    rows_in = got[0].reshape(capacity, n_ex * width_part)
    rows_grad = got[1].reshape(capacity, n_ex * width_part)

    gate_w, up_w, down_w = w_gate[0], w_up[0], w_down[0]
    gate_pre, up_pre, gate_sig, activated, hidden = forward_part(rows_in, gate_w, up_w)
    hidden_delta = jnp.dot(rows_grad, down_w.T, preferred_element_type=jnp.float32)
    down_grad = jnp.dot(hidden.T, rows_grad, preferred_element_type=jnp.float32).astype(
        jnp.bfloat16
    )
    gate_delta = (hidden_delta * up_pre * gate_sig * (1.0 + gate_pre * (1.0 - gate_sig))).astype(
        jnp.bfloat16
    )
    up_delta = (hidden_delta * activated).astype(jnp.bfloat16)
    gate_grad = jnp.dot(rows_in.T, gate_delta, preferred_element_type=jnp.float32).astype(
        jnp.bfloat16
    )
    up_grad = jnp.dot(rows_in.T, up_delta, preferred_element_type=jnp.float32).astype(jnp.bfloat16)
    from_gate = jnp.dot(gate_delta, gate_w.T, preferred_element_type=jnp.float32)
    from_up = jnp.dot(up_delta, up_w.T, preferred_element_type=jnp.float32)
    partial = (from_gate + from_up).reshape(n_class, per_class, n_ex, width_part)
    partial = partial.transpose(0, 2, 1, 3).reshape(n_class * n_ex, per_class, width_part)
    back = lax.all_to_all(partial, LOCAL, 0, 0, tiled=True)
    back = jnp.sum(back.reshape(n_class, n_ex * per_class, width_part), axis=0)
    token_part = jnp.dot(placer_tok.astype(jnp.float32), back, precision=lax.Precision.HIGHEST)
    owned = lax.all_to_all(token_part.reshape(n_z, tok, width_part), "z", 0, 0, tiled=True)
    input_grad = jnp.sum(owned, axis=0).astype(jnp.bfloat16)
    return (input_grad, gate_grad[None], up_grad[None], down_grad[None])


def solution(mesh):
    n_dp, n_ex = mesh.shape["dp"], mesh.shape["expert"]
    fine = Mesh(mesh.devices.reshape(n_dp // 4, 2, 2, 2, n_ex // 2), DP + EX)
    placed = (
        P(DP, EX),
        P(DP, None),
        P(DP, None),
        P(DP, EX),
        P(EX, None, DP),
        P(EX, None, DP),
        P(EX, DP, None),
    )
    return jax.shard_map(
        per_device,
        mesh=fine,
        in_specs=placed,
        out_specs=(
            P(DP, EX),
            P(EX, None, DP),
            P(EX, None, DP),
            P(EX, DP, None),
        ),
        check_vma=False,
    )
```

```python
import jax
import jax.numpy as jnp
from jax import lax
from jax.sharding import Mesh, PartitionSpec as P

MOST = 2
DP = ("z", "y_lo", "core")
EX = ("y_hi", "x")
CLASS = ("y_lo", "core")
LOCAL = CLASS + EX


def forward_part(rows_in, w_gate, w_up):
    gate_pre = jnp.dot(rows_in, w_gate, preferred_element_type=jnp.float32)
    up_pre = jnp.dot(rows_in, w_up, preferred_element_type=jnp.float32)
    gate_sig = jax.nn.sigmoid(gate_pre)
    activated = gate_pre * gate_sig
    hidden = (activated * up_pre).astype(jnp.bfloat16)
    return (gate_pre, up_pre, gate_sig, activated, hidden)


def per_device(inputs, routes, combine, cotangent, w_gate, w_up, w_down):
    tok = inputs.shape[0]
    width_part = inputs.shape[1]
    n_ex = lax.axis_size(EX)
    n_z = lax.axis_size("z")
    n_class = lax.axis_size(CLASS)
    per_class = n_z * MOST
    capacity = n_class * per_class
    slots_in_block = 2 * tok

    scaled = (
        combine.reshape(-1)[:, None] * jnp.repeat(cotangent, 2, axis=0).astype(jnp.float32)
    ).astype(jnp.bfloat16)
    route_row = jnp.zeros((1, width_part), jnp.bfloat16)
    route_row = route_row.at[0, :slots_in_block].set(routes.reshape(-1).astype(jnp.bfloat16))
    packed = jnp.concatenate([inputs, scaled, route_row], axis=0)
    pad_rows = (-packed.shape[0]) % 16
    packed = jnp.pad(packed, ((0, pad_rows), (0, 0)))
    every = jnp.broadcast_to(packed[None], (n_z,) + packed.shape)
    every = lax.all_to_all(every, "z", 0, 0, tiled=True)
    class_in = every[:, :tok, :].reshape(n_z * tok, width_part)
    class_scaled = every[:, tok : 3 * tok, :].reshape(n_z * slots_in_block, width_part)
    class_routes = every[:, 3 * tok, :slots_in_block].astype(jnp.int32)

    onehot = (class_routes[:, :, None] == jnp.arange(n_ex, dtype=jnp.int32)).astype(jnp.int32)
    before = jnp.cumsum(onehot, axis=1) - onehot
    rank = jnp.sum(before * onehot, axis=2)
    block_id = jnp.arange(n_z, dtype=jnp.int32)[:, None]
    column = (class_routes * per_class + block_id * MOST + rank).reshape(-1)
    placer = column[:, None] == jnp.arange(n_ex * per_class, dtype=jnp.int32)[None, :]
    placer_tok = jnp.any(placer.reshape(n_z * tok, 2, n_ex * per_class), axis=1)

    sent_in = jnp.dot(
        placer_tok.astype(jnp.bfloat16).T, class_in, preferred_element_type=jnp.float32
    ).astype(jnp.bfloat16)
    sent_grad = jnp.dot(
        placer.astype(jnp.bfloat16).T, class_scaled, preferred_element_type=jnp.float32
    ).astype(jnp.bfloat16)
    sent = jnp.concatenate([sent_in, sent_grad], axis=1).reshape(n_ex, per_class, 2 * width_part)
    sent = jnp.broadcast_to(sent[None], (n_class,) + sent.shape)
    sent = sent.reshape(n_class * n_ex, per_class, 2 * width_part)
    got = lax.all_to_all(sent, LOCAL, 0, 0, tiled=True)
    got = got.reshape(n_class, n_ex, per_class, 2, width_part).transpose(3, 0, 2, 1, 4)
    rows_in = got[0].reshape(capacity, n_ex * width_part)
    rows_grad = got[1].reshape(capacity, n_ex * width_part)

    gate_w, up_w, down_w = w_gate[0], w_up[0], w_down[0]
    gate_pre, up_pre, gate_sig, activated, hidden = forward_part(rows_in, gate_w, up_w)
    hidden_delta = jnp.dot(rows_grad, down_w.T, preferred_element_type=jnp.float32)
    down_grad = jnp.dot(hidden.T, rows_grad, preferred_element_type=jnp.float32).astype(
        jnp.bfloat16
    )
    gate_delta = (hidden_delta * up_pre * gate_sig * (1.0 + gate_pre * (1.0 - gate_sig))).astype(
        jnp.bfloat16
    )
    up_delta = (hidden_delta * activated).astype(jnp.bfloat16)
    gate_grad = jnp.dot(rows_in.T, gate_delta, preferred_element_type=jnp.float32).astype(
        jnp.bfloat16
    )
    up_grad = jnp.dot(rows_in.T, up_delta, preferred_element_type=jnp.float32).astype(jnp.bfloat16)
    from_gate = jnp.dot(gate_delta, gate_w.T, preferred_element_type=jnp.float32)
    from_up = jnp.dot(up_delta, up_w.T, preferred_element_type=jnp.float32)
    partial = (from_gate + from_up).reshape(n_class, per_class, n_ex, width_part)
    partial = partial.transpose(0, 2, 1, 3).reshape(n_class * n_ex, per_class, width_part)
    back = lax.all_to_all(partial, LOCAL, 0, 0, tiled=True)
    back = jnp.sum(back.reshape(n_class, n_ex * per_class, width_part), axis=0)
    token_part = jnp.dot(placer_tok.astype(jnp.float32), back, precision=lax.Precision.HIGHEST)
    owned = lax.all_to_all(token_part.reshape(n_z, tok, width_part), "z", 0, 0, tiled=True)
    input_grad = jnp.sum(owned, axis=0).astype(jnp.bfloat16)
    return (input_grad, gate_grad[None], up_grad[None], down_grad[None])


def solution(mesh):
    n_dp, n_ex = mesh.shape["dp"], mesh.shape["expert"]
    fine = Mesh(mesh.devices.reshape(n_dp // 4, 2, 2, 2, n_ex // 2), DP + EX)
    placed = (
        P(DP, EX),
        P(DP, None),
        P(DP, None),
        P(DP, EX),
        P(EX, None, DP),
        P(EX, None, DP),
        P(EX, DP, None),
    )
    return jax.shard_map(
        per_device,
        mesh=fine,
        in_specs=placed,
        out_specs=(
            P(DP, EX),
            P(EX, None, DP),
            P(EX, None, DP),
            P(EX, DP, None),
        ),
        check_vma=False,
    )
```

```python
import jax
import jax.numpy as jnp
from jax import lax
from jax.sharding import Mesh, PartitionSpec as P

MOST = 2
DP = ("z", "y_lo", "core")
EX = ("y_hi", "x")
CLASS = ("y_lo", "core")
LOCAL = CLASS + EX


def forward_part(rows_in, w_gate, w_up):
    gate_pre = jnp.dot(rows_in, w_gate, preferred_element_type=jnp.float32)
    up_pre = jnp.dot(rows_in, w_up, preferred_element_type=jnp.float32)
    gate_sig = jax.nn.sigmoid(gate_pre)
    activated = gate_pre * gate_sig
    hidden = (activated * up_pre).astype(jnp.bfloat16)
    return (gate_pre, up_pre, gate_sig, activated, hidden)


def per_device(inputs, routes, combine, cotangent, w_gate, w_up, w_down):
    tok = inputs.shape[0]
    width_part = inputs.shape[1]
    n_ex = lax.axis_size(EX)
    n_z = lax.axis_size("z")
    n_class = lax.axis_size(CLASS)
    per_class = n_z * MOST
    capacity = n_class * per_class
    slots_in_block = 2 * tok

    scaled = (
        combine.reshape(-1)[:, None] * jnp.repeat(cotangent, 2, axis=0).astype(jnp.float32)
    ).astype(jnp.bfloat16)
    route_row = jnp.zeros((1, width_part), jnp.bfloat16)
    route_row = route_row.at[0, :slots_in_block].set(routes.reshape(-1).astype(jnp.bfloat16))
    packed = jnp.concatenate([inputs, scaled, route_row], axis=0)
    pad_rows = (-packed.shape[0]) % 16
    packed = jnp.pad(packed, ((0, pad_rows), (0, 0)))
    every = jnp.broadcast_to(packed[None], (n_z,) + packed.shape)
    every = lax.all_to_all(every, "z", 0, 0, tiled=True)
    class_in = every[:, :tok, :].reshape(n_z * tok, width_part)
    class_scaled = every[:, tok : 3 * tok, :].reshape(n_z * slots_in_block, width_part)
    class_routes = every[:, 3 * tok, :slots_in_block].astype(jnp.int32)

    onehot = (class_routes[:, :, None] == jnp.arange(n_ex, dtype=jnp.int32)).astype(jnp.int32)
    before = jnp.cumsum(onehot, axis=1) - onehot
    rank = jnp.sum(before * onehot, axis=2)
    block_id = jnp.arange(n_z, dtype=jnp.int32)[:, None]
    column = (class_routes * per_class + block_id * MOST + rank).reshape(-1)
    placer = column[:, None] == jnp.arange(n_ex * per_class, dtype=jnp.int32)[None, :]
    placer_tok = jnp.any(placer.reshape(n_z * tok, 2, n_ex * per_class), axis=1)

    sent_in = jnp.dot(
        placer_tok.astype(jnp.bfloat16).T, class_in, preferred_element_type=jnp.float32
    ).astype(jnp.bfloat16)
    sent_grad = jnp.dot(
        placer.astype(jnp.bfloat16).T, class_scaled, preferred_element_type=jnp.float32
    ).astype(jnp.bfloat16)
    sent = jnp.stack(
        [sent_in.reshape(n_ex, per_class, width_part), sent_grad.reshape(n_ex, per_class, width_part)],
        axis=1,
    )
    sent = jnp.broadcast_to(sent[None], (n_class,) + sent.shape)
    sent = sent.reshape(n_class * n_ex, 2, per_class, width_part)
    got = lax.all_to_all(sent, LOCAL, 0, 0, tiled=True)
    got = got.reshape(n_class, n_ex, 2, per_class, width_part).transpose(2, 0, 3, 1, 4)
    rows_in = got[0].reshape(capacity, n_ex * width_part)
    rows_grad = got[1].reshape(capacity, n_ex * width_part)

    gate_w, up_w, down_w = w_gate[0], w_up[0], w_down[0]
    gate_pre, up_pre, gate_sig, activated, hidden = forward_part(rows_in, gate_w, up_w)
    hidden_delta = jnp.dot(rows_grad, down_w.T, preferred_element_type=jnp.float32)
    down_grad = jnp.dot(hidden.T, rows_grad, preferred_element_type=jnp.float32).astype(
        jnp.bfloat16
    )
    gate_delta = (hidden_delta * up_pre * gate_sig * (1.0 + gate_pre * (1.0 - gate_sig))).astype(
        jnp.bfloat16
    )
    up_delta = (hidden_delta * activated).astype(jnp.bfloat16)
    gate_grad = jnp.dot(rows_in.T, gate_delta, preferred_element_type=jnp.float32).astype(
        jnp.bfloat16
    )
    up_grad = jnp.dot(rows_in.T, up_delta, preferred_element_type=jnp.float32).astype(jnp.bfloat16)
    from_gate = jnp.dot(gate_delta, gate_w.T, preferred_element_type=jnp.float32)
    from_up = jnp.dot(up_delta, up_w.T, preferred_element_type=jnp.float32)
    partial = (from_gate + from_up).reshape(n_class, per_class, n_ex, width_part)
    partial = partial.transpose(0, 2, 1, 3).reshape(n_class * n_ex, per_class, width_part)
    back = lax.all_to_all(partial, LOCAL, 0, 0, tiled=True)
    back = jnp.sum(back.reshape(n_class, n_ex * per_class, width_part), axis=0)
    token_part = jnp.dot(placer_tok.astype(jnp.float32), back, precision=lax.Precision.HIGHEST)
    owned = lax.all_to_all(token_part.reshape(n_z, tok, width_part), "z", 0, 0, tiled=True)
    input_grad = jnp.sum(owned, axis=0).astype(jnp.bfloat16)
    return (input_grad, gate_grad[None], up_grad[None], down_grad[None])


def solution(mesh):
    n_dp, n_ex = mesh.shape["dp"], mesh.shape["expert"]
    fine = Mesh(mesh.devices.reshape(n_dp // 4, 2, 2, 2, n_ex // 2), DP + EX)
    placed = (
        P(DP, EX),
        P(DP, None),
        P(DP, None),
        P(DP, EX),
        P(EX, None, DP),
        P(EX, None, DP),
        P(EX, DP, None),
    )
    return jax.shard_map(
        per_device,
        mesh=fine,
        in_specs=placed,
        out_specs=(
            P(DP, EX),
            P(EX, None, DP),
            P(EX, None, DP),
            P(EX, DP, None),
        ),
        check_vma=False,
    )
```

```python
import jax
import jax.numpy as jnp
from jax import lax
from jax.sharding import Mesh, PartitionSpec as P

MOST = 2
DP = ("z", "y_lo", "core")
EX = ("y_hi", "x")
CLASS = ("y_lo", "core")
LOCAL = CLASS + EX


def forward_part(rows_in, w_gate, w_up):
    gate_pre = jnp.dot(rows_in, w_gate, preferred_element_type=jnp.float32)
    up_pre = jnp.dot(rows_in, w_up, preferred_element_type=jnp.float32)
    gate_sig = jax.nn.sigmoid(gate_pre)
    activated = gate_pre * gate_sig
    hidden = (activated * up_pre).astype(jnp.bfloat16)
    return (gate_pre, up_pre, gate_sig, activated, hidden)


def per_device(inputs, routes, combine, cotangent, w_gate, w_up, w_down):
    tok = inputs.shape[0]
    width_part = inputs.shape[1]
    n_ex = lax.axis_size(EX)
    n_z = lax.axis_size("z")
    n_class = lax.axis_size(CLASS)
    per_class = n_z * MOST
    capacity = n_class * per_class
    slots_in_block = 2 * tok

    scaled = (combine[:, :, None] * cotangent[:, None, :].astype(jnp.float32)).astype(jnp.bfloat16)
    scaled = scaled.reshape(slots_in_block, width_part)
    route_row = routes.reshape(1, slots_in_block).astype(jnp.bfloat16)
    route_row = jnp.pad(route_row, ((0, 0), (0, width_part - slots_in_block)))
    pad_rows = (-(3 * tok + 1)) % 16
    packed = jnp.concatenate(
        [inputs, scaled, route_row, jnp.zeros((pad_rows, width_part), jnp.bfloat16)], axis=0
    )
    every = jnp.broadcast_to(packed[None], (n_z,) + packed.shape)
    every = lax.all_to_all(every, "z", 0, 0, tiled=True)
    class_in = every[:, :tok, :].reshape(n_z * tok, width_part)
    class_scaled = every[:, tok : 3 * tok, :].reshape(n_z * slots_in_block, width_part)
    class_routes = every[:, 3 * tok, :slots_in_block].astype(jnp.int32)

    onehot = (class_routes[:, :, None] == jnp.arange(n_ex, dtype=jnp.int32)).astype(jnp.int32)
    before = jnp.cumsum(onehot, axis=1) - onehot
    rank = jnp.sum(before * onehot, axis=2)
    block_id = jnp.arange(n_z, dtype=jnp.int32)[:, None]
    column = (class_routes * per_class + block_id * MOST + rank).reshape(-1)
    placer = column[:, None] == jnp.arange(n_ex * per_class, dtype=jnp.int32)[None, :]
    placer_tok = jnp.any(placer.reshape(n_z * tok, 2, n_ex * per_class), axis=1)

    sent_in = jnp.dot(
        placer_tok.astype(jnp.bfloat16).T, class_in, preferred_element_type=jnp.float32
    ).astype(jnp.bfloat16)
    sent_grad = jnp.dot(
        placer.astype(jnp.bfloat16).T, class_scaled, preferred_element_type=jnp.float32
    ).astype(jnp.bfloat16)
    sent = jnp.stack(
        [sent_in.reshape(n_ex, per_class, width_part), sent_grad.reshape(n_ex, per_class, width_part)],
        axis=1,
    )
    sent = jnp.broadcast_to(sent[None], (n_class,) + sent.shape)
    sent = sent.reshape(n_class * n_ex, 2, per_class, width_part)
    got = lax.all_to_all(sent, LOCAL, 0, 0, tiled=True)
    got = got.reshape(n_class, n_ex, 2, per_class, width_part).transpose(2, 0, 3, 1, 4)
    rows_in = got[0].reshape(capacity, n_ex * width_part)
    rows_grad = got[1].reshape(capacity, n_ex * width_part)

    gate_w, up_w, down_w = w_gate[0], w_up[0], w_down[0]
    gate_pre, up_pre, gate_sig, activated, hidden = forward_part(rows_in, gate_w, up_w)
    hidden_delta = jnp.dot(rows_grad, down_w.T, preferred_element_type=jnp.float32)
    down_grad = jnp.dot(hidden.T, rows_grad, preferred_element_type=jnp.float32).astype(
        jnp.bfloat16
    )
    gate_delta = (hidden_delta * up_pre * gate_sig * (1.0 + gate_pre * (1.0 - gate_sig))).astype(
        jnp.bfloat16
    )
    up_delta = (hidden_delta * activated).astype(jnp.bfloat16)
    gate_grad = jnp.dot(rows_in.T, gate_delta, preferred_element_type=jnp.float32).astype(
        jnp.bfloat16
    )
    up_grad = jnp.dot(rows_in.T, up_delta, preferred_element_type=jnp.float32).astype(jnp.bfloat16)
    by_slice = (n_ex, width_part, gate_w.shape[1])
    from_gate = jnp.einsum(
        "csf,edf->cesd",
        gate_delta.reshape(n_class, per_class, -1),
        gate_w.reshape(by_slice),
        preferred_element_type=jnp.float32,
    )
    from_up = jnp.einsum(
        "csf,edf->cesd",
        up_delta.reshape(n_class, per_class, -1),
        up_w.reshape(by_slice),
        preferred_element_type=jnp.float32,
    )
    partial = (from_gate + from_up).reshape(n_class * n_ex, per_class, width_part)
    back = lax.all_to_all(partial, LOCAL, 0, 0, tiled=True)
    back = back.reshape(n_class * n_ex * per_class, width_part)
    picker = jnp.tile(placer_tok.astype(jnp.float32), (1, n_class))
    token_part = jnp.dot(picker, back, precision=lax.Precision.HIGHEST)
    owned = lax.all_to_all(token_part.reshape(n_z, tok, width_part), "z", 0, 0, tiled=True)
    input_grad = jnp.sum(owned, axis=0).astype(jnp.bfloat16)
    return (input_grad, gate_grad[None], up_grad[None], down_grad[None])


def solution(mesh):
    n_dp, n_ex = mesh.shape["dp"], mesh.shape["expert"]
    fine = Mesh(mesh.devices.reshape(n_dp // 4, 2, 2, 2, n_ex // 2), DP + EX)
    placed = (
        P(DP, EX),
        P(DP, None),
        P(DP, None),
        P(DP, EX),
        P(EX, None, DP),
        P(EX, None, DP),
        P(EX, DP, None),
    )
    return jax.shard_map(
        per_device,
        mesh=fine,
        in_specs=placed,
        out_specs=(
            P(DP, EX),
            P(EX, None, DP),
            P(EX, None, DP),
            P(EX, DP, None),
        ),
        check_vma=False,
    )
```

```python
import jax
import jax.numpy as jnp
from jax import lax
from jax.sharding import Mesh, PartitionSpec as P

MOST = 2
DP = ("z", "y_lo", "core")
EX = ("y_hi", "x")
CLASS = ("y_lo", "core")
LOCAL = CLASS + EX


def forward_part(rows_in, w_gate, w_up):
    gate_pre = jnp.dot(rows_in, w_gate, preferred_element_type=jnp.float32)
    up_pre = jnp.dot(rows_in, w_up, preferred_element_type=jnp.float32)
    gate_sig = jax.nn.sigmoid(gate_pre)
    activated = gate_pre * gate_sig
    hidden = (activated * up_pre).astype(jnp.bfloat16)
    return (gate_pre, up_pre, gate_sig, activated, hidden)


def per_device(inputs, routes, combine, cotangent, w_gate, w_up, w_down):
    tok = inputs.shape[0]
    width_part = inputs.shape[1]
    n_ex = lax.axis_size(EX)
    n_z = lax.axis_size("z")
    n_class = lax.axis_size(CLASS)
    per_class = n_z * MOST
    capacity = n_class * per_class
    slots_in_block = 2 * tok

    scaled = (combine[:, :, None] * cotangent[:, None, :].astype(jnp.float32)).astype(jnp.bfloat16)
    scaled = scaled.reshape(slots_in_block, width_part)
    route_row = routes.reshape(1, slots_in_block).astype(jnp.bfloat16)
    route_row = jnp.pad(route_row, ((0, 0), (0, width_part - slots_in_block)))
    pad_rows = (-(3 * tok + 1)) % 16
    parts = [inputs, scaled, route_row, jnp.zeros((pad_rows, width_part), jnp.bfloat16)]
    every = jnp.concatenate([jnp.broadcast_to(p[None], (n_z,) + p.shape) for p in parts], axis=1)
    every = lax.all_to_all(every, "z", 0, 0, tiled=True)
    class_in = every[:, :tok, :].reshape(n_z * tok, width_part)
    class_scaled = every[:, tok : 3 * tok, :].reshape(n_z * slots_in_block, width_part)
    class_routes = every[:, 3 * tok, :slots_in_block].astype(jnp.int32)

    onehot = (class_routes[:, :, None] == jnp.arange(n_ex, dtype=jnp.int32)).astype(jnp.int32)
    before = jnp.cumsum(onehot, axis=1) - onehot
    rank = jnp.sum(before * onehot, axis=2)
    block_id = jnp.arange(n_z, dtype=jnp.int32)[:, None]
    column = (class_routes * per_class + block_id * MOST + rank).reshape(-1)
    placer = column[:, None] == jnp.arange(n_ex * per_class, dtype=jnp.int32)[None, :]
    placer_tok = jnp.any(placer.reshape(n_z * tok, 2, n_ex * per_class), axis=1)

    sent_in = jnp.dot(
        placer_tok.astype(jnp.bfloat16).T, class_in, preferred_element_type=jnp.float32
    ).astype(jnp.bfloat16)
    sent_grad = jnp.dot(
        placer.astype(jnp.bfloat16).T, class_scaled, preferred_element_type=jnp.float32
    ).astype(jnp.bfloat16)
    sent = jnp.stack(
        [sent_in.reshape(n_ex, per_class, width_part), sent_grad.reshape(n_ex, per_class, width_part)],
        axis=1,
    )
    sent = jnp.broadcast_to(sent[None], (n_class,) + sent.shape)
    sent = sent.reshape(n_class * n_ex, 2, per_class, width_part)
    got = lax.all_to_all(sent, LOCAL, 0, 0, tiled=True)
    got = got.reshape(n_class, n_ex, 2, per_class, width_part).transpose(2, 0, 3, 1, 4)
    rows_in = got[0].reshape(capacity, n_ex * width_part)
    rows_grad = got[1].reshape(capacity, n_ex * width_part)

    gate_w, up_w, down_w = w_gate[0], w_up[0], w_down[0]
    gate_pre, up_pre, gate_sig, activated, hidden = forward_part(rows_in, gate_w, up_w)
    hidden_delta = jnp.dot(rows_grad, down_w.T, preferred_element_type=jnp.float32)
    down_grad = jnp.dot(hidden.T, rows_grad, preferred_element_type=jnp.float32).astype(
        jnp.bfloat16
    )
    gate_delta = (hidden_delta * up_pre * gate_sig * (1.0 + gate_pre * (1.0 - gate_sig))).astype(
        jnp.bfloat16
    )
    up_delta = (hidden_delta * activated).astype(jnp.bfloat16)
    gate_grad = jnp.dot(rows_in.T, gate_delta, preferred_element_type=jnp.float32).astype(
        jnp.bfloat16
    )
    up_grad = jnp.dot(rows_in.T, up_delta, preferred_element_type=jnp.float32).astype(jnp.bfloat16)
    by_slice = (n_ex, width_part, gate_w.shape[1])
    from_gate = jnp.einsum(
        "csf,edf->cesd",
        gate_delta.reshape(n_class, per_class, -1),
        gate_w.reshape(by_slice),
        preferred_element_type=jnp.float32,
    )
    from_up = jnp.einsum(
        "csf,edf->cesd",
        up_delta.reshape(n_class, per_class, -1),
        up_w.reshape(by_slice),
        preferred_element_type=jnp.float32,
    )
    partial = (from_gate + from_up).reshape(n_class * n_ex, per_class, width_part)
    back = lax.all_to_all(partial, LOCAL, 0, 0, tiled=True)
    back = jnp.sum(back.reshape(n_class, n_ex * per_class, width_part), axis=0)
    token_part = jnp.take(back, column, axis=0, mode="clip")
    token_part = jnp.sum(token_part.reshape(n_z * tok, 2, width_part), axis=1)
    owned = lax.all_to_all(token_part.reshape(n_z, tok, width_part), "z", 0, 0, tiled=True)
    input_grad = jnp.sum(owned, axis=0).astype(jnp.bfloat16)
    return (input_grad, gate_grad[None], up_grad[None], down_grad[None])


def solution(mesh):
    n_dp, n_ex = mesh.shape["dp"], mesh.shape["expert"]
    fine = Mesh(mesh.devices.reshape(n_dp // 4, 2, 2, 2, n_ex // 2), DP + EX)
    placed = (
        P(DP, EX),
        P(DP, None),
        P(DP, None),
        P(DP, EX),
        P(EX, None, DP),
        P(EX, None, DP),
        P(EX, DP, None),
    )
    return jax.shard_map(
        per_device,
        mesh=fine,
        in_specs=placed,
        out_specs=(
            P(DP, EX),
            P(EX, None, DP),
            P(EX, None, DP),
            P(EX, DP, None),
        ),
        check_vma=False,
    )
```

```python
import jax
import jax.numpy as jnp
from jax import lax
from jax.sharding import Mesh, PartitionSpec as P

MOST = 2
DP = ("z", "y_lo", "core")
EX = ("y_hi", "x")
CLASS = ("y_lo", "core")
LOCAL = CLASS + EX


def forward_part(rows_in, w_gate, w_up):
    gate_pre = jnp.dot(rows_in, w_gate, preferred_element_type=jnp.float32)
    up_pre = jnp.dot(rows_in, w_up, preferred_element_type=jnp.float32)
    gate_sig = jax.nn.sigmoid(gate_pre)
    activated = gate_pre * gate_sig
    hidden = (activated * up_pre).astype(jnp.bfloat16)
    return (gate_pre, up_pre, gate_sig, activated, hidden)


def per_device(inputs, routes, combine, cotangent, w_gate, w_up, w_down):
    tok = inputs.shape[0]
    width_part = inputs.shape[1]
    n_ex = lax.axis_size(EX)
    n_z = lax.axis_size("z")
    n_class = lax.axis_size(CLASS)
    per_class = n_z * MOST
    capacity = n_class * per_class
    slots_in_block = 2 * tok

    scaled = (combine.T[:, :, None] * cotangent[None, :, :].astype(jnp.float32)).astype(jnp.bfloat16)
    scaled = scaled.reshape(slots_in_block, width_part)
    route_row = routes.T.reshape(1, slots_in_block).astype(jnp.bfloat16)
    route_row = jnp.pad(route_row, ((0, 0), (0, width_part - slots_in_block)))
    pad_rows = (-(3 * tok + 1)) % 16
    packed = jnp.concatenate(
        [inputs, scaled, route_row, jnp.zeros((pad_rows, width_part), jnp.bfloat16)], axis=0
    )
    every = jnp.broadcast_to(packed[None], (n_z,) + packed.shape)
    every = lax.all_to_all(every, "z", 0, 0, tiled=True)
    class_in = every[:, :tok, :].reshape(n_z * tok, width_part)
    class_scaled = every[:, tok : 3 * tok, :].reshape(n_z * slots_in_block, width_part)
    class_routes = every[:, 3 * tok, :slots_in_block].astype(jnp.int32)

    onehot = (class_routes[:, :, None] == jnp.arange(n_ex, dtype=jnp.int32)).astype(jnp.int32)
    before = jnp.cumsum(onehot, axis=1) - onehot
    rank = jnp.sum(before * onehot, axis=2)
    block_id = jnp.arange(n_z, dtype=jnp.int32)[:, None]
    column = (class_routes * per_class + block_id * MOST + rank).reshape(-1)
    placer = column[:, None] == jnp.arange(n_ex * per_class, dtype=jnp.int32)[None, :]
    placer_tok = jnp.any(placer.reshape(n_z, 2, tok, n_ex * per_class), axis=1)
    placer_tok = placer_tok.reshape(n_z * tok, n_ex * per_class)

    sent_in = jnp.dot(
        placer_tok.astype(jnp.bfloat16).T, class_in, preferred_element_type=jnp.float32
    ).astype(jnp.bfloat16)
    sent_grad = jnp.dot(
        placer.astype(jnp.bfloat16).T, class_scaled, preferred_element_type=jnp.float32
    ).astype(jnp.bfloat16)
    sent = jnp.stack(
        [sent_in.reshape(n_ex, per_class, width_part), sent_grad.reshape(n_ex, per_class, width_part)],
        axis=1,
    )
    sent = jnp.broadcast_to(sent[None], (n_class,) + sent.shape)
    sent = sent.reshape(n_class * n_ex, 2, per_class, width_part)
    got = lax.all_to_all(sent, LOCAL, 0, 0, tiled=True)
    got = got.reshape(n_class, n_ex, 2, per_class, width_part).transpose(2, 0, 3, 1, 4)
    rows_in = got[0].reshape(capacity, n_ex * width_part)
    rows_grad = got[1].reshape(capacity, n_ex * width_part)

    gate_w, up_w, down_w = w_gate[0], w_up[0], w_down[0]
    gate_pre, up_pre, gate_sig, activated, hidden = forward_part(rows_in, gate_w, up_w)
    hidden_delta = jnp.dot(rows_grad, down_w.T, preferred_element_type=jnp.float32)
    down_grad = jnp.dot(hidden.T, rows_grad, preferred_element_type=jnp.float32).astype(
        jnp.bfloat16
    )
    gate_delta = (hidden_delta * up_pre * gate_sig * (1.0 + gate_pre * (1.0 - gate_sig))).astype(
        jnp.bfloat16
    )
    up_delta = (hidden_delta * activated).astype(jnp.bfloat16)
    gate_grad = jnp.dot(rows_in.T, gate_delta, preferred_element_type=jnp.float32).astype(
        jnp.bfloat16
    )
    up_grad = jnp.dot(rows_in.T, up_delta, preferred_element_type=jnp.float32).astype(jnp.bfloat16)
    by_slice = (n_ex, width_part, gate_w.shape[1])
    from_gate = jnp.einsum(
        "csf,edf->cesd",
        gate_delta.reshape(n_class, per_class, -1),
        gate_w.reshape(by_slice),
        preferred_element_type=jnp.float32,
    )
    from_up = jnp.einsum(
        "csf,edf->cesd",
        up_delta.reshape(n_class, per_class, -1),
        up_w.reshape(by_slice),
        preferred_element_type=jnp.float32,
    )
    partial = (from_gate + from_up).reshape(n_class * n_ex, per_class, width_part)
    back = lax.all_to_all(partial, LOCAL, 0, 0, tiled=True)
    back = back.reshape(n_class * n_ex * per_class, width_part)
    picker = jnp.tile(placer_tok.astype(jnp.float32), (1, n_class))
    token_part = jnp.dot(picker, back, precision=lax.Precision.HIGHEST)
    owned = lax.all_to_all(token_part.reshape(n_z, tok, width_part), "z", 0, 0, tiled=True)
    input_grad = jnp.sum(owned, axis=0).astype(jnp.bfloat16)
    return (input_grad, gate_grad[None], up_grad[None], down_grad[None])


def solution(mesh):
    n_dp, n_ex = mesh.shape["dp"], mesh.shape["expert"]
    fine = Mesh(mesh.devices.reshape(n_dp // 4, 2, 2, 2, n_ex // 2), DP + EX)
    placed = (
        P(DP, EX),
        P(DP, None),
        P(DP, None),
        P(DP, EX),
        P(EX, None, DP),
        P(EX, None, DP),
        P(EX, DP, None),
    )
    return jax.shard_map(
        per_device,
        mesh=fine,
        in_specs=placed,
        out_specs=(
            P(DP, EX),
            P(EX, None, DP),
            P(EX, None, DP),
            P(EX, DP, None),
        ),
        check_vma=False,
    )
```

```python
import jax
import jax.numpy as jnp
from jax import lax
from jax.experimental import pallas as pl
from jax.experimental.pallas import tpu as pltpu
from jax.sharding import Mesh, PartitionSpec as P

MOST = 2
DP = ("z", "y_lo", "core")
EX = ("y_hi", "x")
CLASS = ("y_lo", "core")
LOCAL = CLASS + EX


def forward_part(rows_in, w_gate, w_up):
    gate_pre = jnp.dot(rows_in, w_gate, preferred_element_type=jnp.float32)
    up_pre = jnp.dot(rows_in, w_up, preferred_element_type=jnp.float32)
    gate_sig = jax.nn.sigmoid(gate_pre)
    activated = gate_pre * gate_sig
    hidden = (activated * up_pre).astype(jnp.bfloat16)
    return (gate_pre, up_pre, gate_sig, activated, hidden)


def pack_kernel(x_ref, cot_ref, comb_ref, rt_ref, o_ref, rows_ref):
    tok, width = x_ref.shape
    rows_ref[...] = jnp.zeros(rows_ref.shape, jnp.float32)
    rows_ref[0:tok, :] = x_ref[...].astype(jnp.float32)
    cot = cot_ref[...].astype(jnp.float32)
    lane = lax.broadcasted_iota(jnp.int32, (1, width), 1)
    route_row = jnp.zeros((1, width), jnp.float32)
    for k in range(2):
        for t in range(tok):
            a = k * tok + t
            row = (comb_ref[k, t] * cot[t : t + 1, :]).astype(jnp.bfloat16)
            rows_ref[tok + a : tok + a + 1, :] = row.astype(jnp.float32)
            route_row = jnp.where(lane == a, rt_ref[k, t].astype(jnp.float32), route_row)
    rows_ref[3 * tok : 3 * tok + 1, :] = route_row
    packed = rows_ref[...].astype(jnp.bfloat16)
    for z in range(o_ref.shape[0]):
        o_ref[z] = packed


def pack_block(inputs, cotangent, weights, routes, copies):
    tok, width = inputs.shape
    rows = 3 * tok + 1 + (-(3 * tok + 1)) % 16
    vmem = pl.BlockSpec(memory_space=pltpu.VMEM)
    smem = pl.BlockSpec(memory_space=pltpu.SMEM)
    return pl.pallas_call(
        pack_kernel,
        out_shape=jax.ShapeDtypeStruct((copies, rows, width), jnp.bfloat16),
        in_specs=[vmem, vmem, smem, smem],
        out_specs=vmem,
        scratch_shapes=[pltpu.VMEM((rows, width), jnp.float32)],
    )(inputs, cotangent, weights, routes)


def per_device(inputs, routes, combine, cotangent, w_gate, w_up, w_down):
    tok = inputs.shape[0]
    width_part = inputs.shape[1]
    n_ex = lax.axis_size(EX)
    n_z = lax.axis_size("z")
    n_class = lax.axis_size(CLASS)
    per_class = n_z * MOST
    capacity = n_class * per_class
    slots_in_block = 2 * tok

    every = pack_block(inputs, cotangent, combine.T, routes.T, n_z)
    every = lax.all_to_all(every, "z", 0, 0, tiled=True)
    class_in = every[:, :tok, :].reshape(n_z * tok, width_part)
    class_scaled = every[:, tok : 3 * tok, :].reshape(n_z * slots_in_block, width_part)
    class_routes = every[:, 3 * tok, :slots_in_block].astype(jnp.int32)

    onehot = (class_routes[:, :, None] == jnp.arange(n_ex, dtype=jnp.int32)).astype(jnp.int32)
    before = jnp.cumsum(onehot, axis=1) - onehot
    rank = jnp.sum(before * onehot, axis=2)
    block_id = jnp.arange(n_z, dtype=jnp.int32)[:, None]
    column = (class_routes * per_class + block_id * MOST + rank).reshape(-1)
    placer = column[:, None] == jnp.arange(n_ex * per_class, dtype=jnp.int32)[None, :]
    placer_tok = jnp.any(placer.reshape(n_z, 2, tok, n_ex * per_class), axis=1)
    placer_tok = placer_tok.reshape(n_z * tok, n_ex * per_class)

    sent_in = jnp.dot(
        placer_tok.astype(jnp.bfloat16).T, class_in, preferred_element_type=jnp.float32
    ).astype(jnp.bfloat16)
    sent_grad = jnp.dot(
        placer.astype(jnp.bfloat16).T, class_scaled, preferred_element_type=jnp.float32
    ).astype(jnp.bfloat16)
    sent = jnp.stack(
        [sent_in.reshape(n_ex, per_class, width_part), sent_grad.reshape(n_ex, per_class, width_part)],
        axis=1,
    )
    sent = jnp.broadcast_to(sent[None], (n_class,) + sent.shape)
    sent = sent.reshape(n_class * n_ex, 2, per_class, width_part)
    got = lax.all_to_all(sent, LOCAL, 0, 0, tiled=True)
    got = got.reshape(n_class, n_ex, 2, per_class, width_part).transpose(2, 0, 3, 1, 4)
    rows_in = got[0].reshape(capacity, n_ex * width_part)
    rows_grad = got[1].reshape(capacity, n_ex * width_part)

    gate_w, up_w, down_w = w_gate[0], w_up[0], w_down[0]
    gate_pre, up_pre, gate_sig, activated, hidden = forward_part(rows_in, gate_w, up_w)
    hidden_delta = jnp.dot(rows_grad, down_w.T, preferred_element_type=jnp.float32)
    down_grad = jnp.dot(hidden.T, rows_grad, preferred_element_type=jnp.float32).astype(
        jnp.bfloat16
    )
    gate_delta = (hidden_delta * up_pre * gate_sig * (1.0 + gate_pre * (1.0 - gate_sig))).astype(
        jnp.bfloat16
    )
    up_delta = (hidden_delta * activated).astype(jnp.bfloat16)
    gate_grad = jnp.dot(rows_in.T, gate_delta, preferred_element_type=jnp.float32).astype(
        jnp.bfloat16
    )
    up_grad = jnp.dot(rows_in.T, up_delta, preferred_element_type=jnp.float32).astype(jnp.bfloat16)
    by_slice = (n_ex, width_part, gate_w.shape[1])
    from_gate = jnp.einsum(
        "csf,edf->cesd",
        gate_delta.reshape(n_class, per_class, -1),
        gate_w.reshape(by_slice),
        preferred_element_type=jnp.float32,
    )
    from_up = jnp.einsum(
        "csf,edf->cesd",
        up_delta.reshape(n_class, per_class, -1),
        up_w.reshape(by_slice),
        preferred_element_type=jnp.float32,
    )
    partial = (from_gate + from_up).reshape(n_class * n_ex, per_class, width_part)
    back = lax.all_to_all(partial, LOCAL, 0, 0, tiled=True)
    back = back.reshape(n_class * n_ex * per_class, width_part)
    picker = jnp.tile(placer_tok.astype(jnp.float32), (1, n_class))
    token_part = jnp.dot(picker, back, precision=lax.Precision.HIGHEST)
    owned = lax.all_to_all(token_part.reshape(n_z, tok, width_part), "z", 0, 0, tiled=True)
    input_grad = jnp.sum(owned, axis=0).astype(jnp.bfloat16)
    return (input_grad, gate_grad[None], up_grad[None], down_grad[None])


def solution(mesh):
    n_dp, n_ex = mesh.shape["dp"], mesh.shape["expert"]
    fine = Mesh(mesh.devices.reshape(n_dp // 4, 2, 2, 2, n_ex // 2), DP + EX)
    placed = (
        P(DP, EX),
        P(DP, None),
        P(DP, None),
        P(DP, EX),
        P(EX, None, DP),
        P(EX, None, DP),
        P(EX, DP, None),
    )
    return jax.shard_map(
        per_device,
        mesh=fine,
        in_specs=placed,
        out_specs=(
            P(DP, EX),
            P(EX, None, DP),
            P(EX, None, DP),
            P(EX, DP, None),
        ),
        check_vma=False,
    )
```

```python
import jax
import jax.numpy as jnp
from jax import lax
from jax.experimental import pallas as pl
from jax.experimental.pallas import tpu as pltpu
from jax.sharding import Mesh, PartitionSpec as P

MOST = 2
DP = ("z", "y_lo", "core")
EX = ("y_hi", "x")
CLASS = ("y_lo", "core")
LOCAL = CLASS + EX


def forward_part(rows_in, w_gate, w_up):
    gate_pre = jnp.dot(rows_in, w_gate, preferred_element_type=jnp.float32)
    up_pre = jnp.dot(rows_in, w_up, preferred_element_type=jnp.float32)
    gate_sig = jax.nn.sigmoid(gate_pre)
    activated = gate_pre * gate_sig
    hidden = (activated * up_pre).astype(jnp.bfloat16)
    return (gate_pre, up_pre, gate_sig, activated, hidden)


def pack_kernel(x_ref, cot_ref, comb_ref, rt_ref, o_ref, rows_ref):
    tok, width = x_ref.shape
    rows_ref[...] = jnp.zeros(rows_ref.shape, jnp.float32)
    rows_ref[0:tok, :] = x_ref[...].astype(jnp.float32)
    cot = cot_ref[...].astype(jnp.float32)
    lane = lax.broadcasted_iota(jnp.int32, (1, width), 1)
    route_row = jnp.zeros((1, width), jnp.float32)
    for k in range(2):
        for t in range(tok):
            a = k * tok + t
            row = (comb_ref[k, t] * cot[t : t + 1, :]).astype(jnp.bfloat16)
            rows_ref[tok + a : tok + a + 1, :] = row.astype(jnp.float32)
            route_row = jnp.where(lane == a, rt_ref[k, t].astype(jnp.float32), route_row)
    rows_ref[3 * tok : 3 * tok + 1, :] = route_row
    packed = rows_ref[...].astype(jnp.bfloat16)
    for z in range(o_ref.shape[0]):
        o_ref[z] = packed


def pack_block(inputs, cotangent, weights, routes, copies):
    tok, width = inputs.shape
    rows = 3 * tok + 1 + (-(3 * tok + 1)) % 16
    vmem = pl.BlockSpec(memory_space=pltpu.VMEM)
    smem = pl.BlockSpec(memory_space=pltpu.SMEM)
    return pl.pallas_call(
        pack_kernel,
        out_shape=jax.ShapeDtypeStruct((copies, rows, width), jnp.bfloat16),
        in_specs=[vmem, vmem, smem, smem],
        out_specs=vmem,
        scratch_shapes=[pltpu.VMEM((rows, width), jnp.float32)],
    )(inputs, cotangent, weights, routes)


def combine_kernel(back_ref, col_ref, o_ref, sum_ref):
    total = back_ref[0]
    for c in range(1, back_ref.shape[0]):
        total = total + back_ref[c]
    sum_ref[...] = total
    n_z, tok, width = o_ref.shape

    def block(zz, carry):
        for t in range(tok):
            acc = jnp.zeros((1, width), jnp.float32)
            for k in range(2):
                col = col_ref[zz * 2 * tok + k * tok + t]
                acc = acc + sum_ref[pl.ds(col, 1), :]
            o_ref[zz, pl.ds(t, 1), :] = acc
        return carry

    lax.fori_loop(0, n_z, block, 0)


def combine_tokens(back, column, n_z, tok):
    vmem = pl.BlockSpec(memory_space=pltpu.VMEM)
    smem = pl.BlockSpec(memory_space=pltpu.SMEM)
    return pl.pallas_call(
        combine_kernel,
        out_shape=jax.ShapeDtypeStruct((n_z, tok, back.shape[2]), jnp.float32),
        in_specs=[vmem, smem],
        out_specs=vmem,
        scratch_shapes=[pltpu.VMEM(back.shape[1:], jnp.float32)],
    )(back, column)


def per_device(inputs, routes, combine, cotangent, w_gate, w_up, w_down):
    tok = inputs.shape[0]
    width_part = inputs.shape[1]
    n_ex = lax.axis_size(EX)
    n_z = lax.axis_size("z")
    n_class = lax.axis_size(CLASS)
    per_class = n_z * MOST
    capacity = n_class * per_class
    slots_in_block = 2 * tok

    every = pack_block(inputs, cotangent, combine.T, routes.T, n_z)
    every = lax.all_to_all(every, "z", 0, 0, tiled=True)
    class_in = every[:, :tok, :].reshape(n_z * tok, width_part)
    class_scaled = every[:, tok : 3 * tok, :].reshape(n_z * slots_in_block, width_part)
    class_routes = every[:, 3 * tok, :slots_in_block].astype(jnp.int32)

    onehot = (class_routes[:, :, None] == jnp.arange(n_ex, dtype=jnp.int32)).astype(jnp.int32)
    before = jnp.cumsum(onehot, axis=1) - onehot
    rank = jnp.sum(before * onehot, axis=2)
    block_id = jnp.arange(n_z, dtype=jnp.int32)[:, None]
    column = (class_routes * per_class + block_id * MOST + rank).reshape(-1)
    placer = column[:, None] == jnp.arange(n_ex * per_class, dtype=jnp.int32)[None, :]
    placer_tok = jnp.any(placer.reshape(n_z, 2, tok, n_ex * per_class), axis=1)
    placer_tok = placer_tok.reshape(n_z * tok, n_ex * per_class)

    sent_in = jnp.dot(
        placer_tok.astype(jnp.bfloat16).T, class_in, preferred_element_type=jnp.float32
    ).astype(jnp.bfloat16)
    sent_grad = jnp.dot(
        placer.astype(jnp.bfloat16).T, class_scaled, preferred_element_type=jnp.float32
    ).astype(jnp.bfloat16)
    sent = jnp.stack(
        [sent_in.reshape(n_ex, per_class, width_part), sent_grad.reshape(n_ex, per_class, width_part)],
        axis=1,
    )
    sent = jnp.broadcast_to(sent[None], (n_class,) + sent.shape)
    sent = sent.reshape(n_class * n_ex, 2, per_class, width_part)
    got = lax.all_to_all(sent, LOCAL, 0, 0, tiled=True)
    got = got.reshape(n_class, n_ex, 2, per_class, width_part).transpose(2, 0, 3, 1, 4)
    rows_in = got[0].reshape(capacity, n_ex * width_part)
    rows_grad = got[1].reshape(capacity, n_ex * width_part)

    gate_w, up_w, down_w = w_gate[0], w_up[0], w_down[0]
    gate_pre, up_pre, gate_sig, activated, hidden = forward_part(rows_in, gate_w, up_w)
    hidden_delta = jnp.dot(rows_grad, down_w.T, preferred_element_type=jnp.float32)
    down_grad = jnp.dot(hidden.T, rows_grad, preferred_element_type=jnp.float32).astype(
        jnp.bfloat16
    )
    gate_delta = (hidden_delta * up_pre * gate_sig * (1.0 + gate_pre * (1.0 - gate_sig))).astype(
        jnp.bfloat16
    )
    up_delta = (hidden_delta * activated).astype(jnp.bfloat16)
    gate_grad = jnp.dot(rows_in.T, gate_delta, preferred_element_type=jnp.float32).astype(
        jnp.bfloat16
    )
    up_grad = jnp.dot(rows_in.T, up_delta, preferred_element_type=jnp.float32).astype(jnp.bfloat16)
    by_slice = (n_ex, width_part, gate_w.shape[1])
    from_gate = jnp.einsum(
        "csf,edf->cesd",
        gate_delta.reshape(n_class, per_class, -1),
        gate_w.reshape(by_slice),
        preferred_element_type=jnp.float32,
    )
    from_up = jnp.einsum(
        "csf,edf->cesd",
        up_delta.reshape(n_class, per_class, -1),
        up_w.reshape(by_slice),
        preferred_element_type=jnp.float32,
    )
    partial = (from_gate + from_up).reshape(n_class * n_ex, per_class, width_part)
    back = lax.all_to_all(partial, LOCAL, 0, 0, tiled=True)
    back = back.reshape(n_class, n_ex * per_class, width_part)
    token_part = combine_tokens(back, column, n_z, tok)
    owned = lax.all_to_all(token_part, "z", 0, 0, tiled=True)
    input_grad = jnp.sum(owned, axis=0).astype(jnp.bfloat16)
    return (input_grad, gate_grad[None], up_grad[None], down_grad[None])


def solution(mesh):
    n_dp, n_ex = mesh.shape["dp"], mesh.shape["expert"]
    fine = Mesh(mesh.devices.reshape(n_dp // 4, 2, 2, 2, n_ex // 2), DP + EX)
    placed = (
        P(DP, EX),
        P(DP, None),
        P(DP, None),
        P(DP, EX),
        P(EX, None, DP),
        P(EX, None, DP),
        P(EX, DP, None),
    )
    return jax.shard_map(
        per_device,
        mesh=fine,
        in_specs=placed,
        out_specs=(
            P(DP, EX),
            P(EX, None, DP),
            P(EX, None, DP),
            P(EX, DP, None),
        ),
        check_vma=False,
    )
```

```python
import jax
import jax.numpy as jnp
from jax import lax
from jax.experimental import pallas as pl
from jax.experimental.pallas import tpu as pltpu
from jax.sharding import Mesh, PartitionSpec as P

MOST = 2
DP = ("z", "y_lo", "core")
EX = ("y_hi", "x")
CLASS = ("y_lo", "core")
LOCAL = CLASS + EX


def forward_part(rows_in, w_gate, w_up):
    gate_pre = jnp.dot(rows_in, w_gate, preferred_element_type=jnp.float32)
    up_pre = jnp.dot(rows_in, w_up, preferred_element_type=jnp.float32)
    gate_sig = jax.nn.sigmoid(gate_pre)
    activated = gate_pre * gate_sig
    hidden = (activated * up_pre).astype(jnp.bfloat16)
    return (gate_pre, up_pre, gate_sig, activated, hidden)


def pack_kernel(x_ref, cot_ref, comb_ref, rt_ref, o_ref, rows_ref):
    tok, width = x_ref.shape
    rows_ref[...] = jnp.zeros(rows_ref.shape, jnp.float32)
    rows_ref[0:tok, :] = x_ref[...].astype(jnp.float32)
    cot = cot_ref[...].astype(jnp.float32)
    lane = lax.broadcasted_iota(jnp.int32, (1, width), 1)
    route_row = jnp.zeros((1, width), jnp.float32)
    for k in range(2):
        for t in range(tok):
            a = k * tok + t
            row = (comb_ref[k, t] * cot[t : t + 1, :]).astype(jnp.bfloat16)
            rows_ref[tok + a : tok + a + 1, :] = row.astype(jnp.float32)
            route_row = jnp.where(lane == a, rt_ref[k, t].astype(jnp.float32), route_row)
    rows_ref[3 * tok : 3 * tok + 1, :] = route_row
    packed = rows_ref[...].astype(jnp.bfloat16)
    for z in range(o_ref.shape[0]):
        o_ref[z] = packed


def pack_block(inputs, cotangent, weights, routes, copies):
    tok, width = inputs.shape
    rows = 3 * tok + 1 + (-(3 * tok + 1)) % 16
    vmem = pl.BlockSpec(memory_space=pltpu.VMEM)
    smem = pl.BlockSpec(memory_space=pltpu.SMEM)
    return pl.pallas_call(
        pack_kernel,
        out_shape=jax.ShapeDtypeStruct((copies, rows, width), jnp.bfloat16),
        in_specs=[vmem, vmem, smem, smem],
        out_specs=vmem,
        scratch_shapes=[pltpu.VMEM((rows, width), jnp.float32)],
    )(inputs, cotangent, weights, routes)


def combine_kernel(back_ref, col_ref, o_ref, sum_ref):
    total = back_ref[0]
    for c in range(1, back_ref.shape[0]):
        total = total + back_ref[c]
    sum_ref[...] = total
    n_z, tok, width = o_ref.shape

    def block(zz, carry):
        for t in range(tok):
            acc = jnp.zeros((1, width), jnp.float32)
            for k in range(2):
                col = col_ref[zz * 2 * tok + k * tok + t]
                acc = acc + sum_ref[pl.ds(col, 1), :]
            o_ref[zz, pl.ds(t, 1), :] = acc
        return carry

    lax.fori_loop(0, n_z, block, 0)


def combine_tokens(back, column, n_z, tok):
    vmem = pl.BlockSpec(memory_space=pltpu.VMEM)
    smem = pl.BlockSpec(memory_space=pltpu.SMEM)
    return pl.pallas_call(
        combine_kernel,
        out_shape=jax.ShapeDtypeStruct((n_z, tok, back.shape[2]), jnp.float32),
        in_specs=[vmem, smem],
        out_specs=vmem,
        scratch_shapes=[pltpu.VMEM(back.shape[1:], jnp.float32)],
    )(back, column)


def row_kernel(got_ref, gw_ref, uw_ref, dw_ref, part_ref, hid_ref, gd_ref, ud_ref):
    n_src, _, rows, width = got_ref.shape
    n_ex = gw_ref.shape[0] // width
    nt = (((1,), (1,)), ((), ()))
    for c in range(n_src // n_ex):
        gate_pre = up_pre = hidden_delta = None
        for e in range(n_ex):
            x_in = got_ref[c * n_ex + e, 0]
            x_grad = got_ref[c * n_ex + e, 1]
            span = slice(e * width, (e + 1) * width)
            g = jnp.dot(x_in, gw_ref[span, :], preferred_element_type=jnp.float32)
            u = jnp.dot(x_in, uw_ref[span, :], preferred_element_type=jnp.float32)
            h = lax.dot_general(x_grad, dw_ref[:, span], nt, preferred_element_type=jnp.float32)
            if e == 0:
                gate_pre, up_pre, hidden_delta = g, u, h
            else:
                gate_pre, up_pre, hidden_delta = gate_pre + g, up_pre + u, hidden_delta + h
        gate_sig = jax.nn.sigmoid(gate_pre)
        activated = gate_pre * gate_sig
        hid_ref[c * rows : (c + 1) * rows, :] = (activated * up_pre).astype(jnp.bfloat16)
        gate_delta = (
            hidden_delta * up_pre * gate_sig * (1.0 + gate_pre * (1.0 - gate_sig))
        ).astype(jnp.bfloat16)
        up_delta = (hidden_delta * activated).astype(jnp.bfloat16)
        gd_ref[c * rows : (c + 1) * rows, :] = gate_delta
        ud_ref[c * rows : (c + 1) * rows, :] = up_delta
        for e in range(n_ex):
            span = slice(e * width, (e + 1) * width)
            part_ref[c * n_ex + e] = lax.dot_general(
                gate_delta, gw_ref[span, :], nt, preferred_element_type=jnp.float32
            ) + lax.dot_general(up_delta, uw_ref[span, :], nt, preferred_element_type=jnp.float32)


def row_math(got, gate_w, up_w, down_w, n_class, n_ex):
    n_src, _, rows, width = got.shape
    ff = gate_w.shape[1]
    vmem = pl.BlockSpec(memory_space=pltpu.VMEM)
    small = jax.ShapeDtypeStruct((n_class * rows, ff), jnp.bfloat16)
    return pl.pallas_call(
        row_kernel,
        out_shape=(jax.ShapeDtypeStruct((n_src, rows, width), jnp.float32), small, small, small),
        in_specs=[vmem] * 4,
        out_specs=(vmem, vmem, vmem, vmem),
    )(got, gate_w, up_w, down_w)


def per_device(inputs, routes, combine, cotangent, w_gate, w_up, w_down):
    tok = inputs.shape[0]
    width_part = inputs.shape[1]
    n_ex = lax.axis_size(EX)
    n_z = lax.axis_size("z")
    n_class = lax.axis_size(CLASS)
    per_class = n_z * MOST
    capacity = n_class * per_class
    slots_in_block = 2 * tok

    every = pack_block(inputs, cotangent, combine.T, routes.T, n_z)
    every = lax.all_to_all(every, "z", 0, 0, tiled=True)
    class_in = every[:, :tok, :].reshape(n_z * tok, width_part)
    class_scaled = every[:, tok : 3 * tok, :].reshape(n_z * slots_in_block, width_part)
    class_routes = every[:, 3 * tok, :slots_in_block].astype(jnp.int32)

    onehot = (class_routes[:, :, None] == jnp.arange(n_ex, dtype=jnp.int32)).astype(jnp.int32)
    before = jnp.cumsum(onehot, axis=1) - onehot
    rank = jnp.sum(before * onehot, axis=2)
    block_id = jnp.arange(n_z, dtype=jnp.int32)[:, None]
    column = (class_routes * per_class + block_id * MOST + rank).reshape(-1)
    placer = column[:, None] == jnp.arange(n_ex * per_class, dtype=jnp.int32)[None, :]
    placer_tok = jnp.any(placer.reshape(n_z, 2, tok, n_ex * per_class), axis=1)
    placer_tok = placer_tok.reshape(n_z * tok, n_ex * per_class)

    sent_in = jnp.dot(
        placer_tok.astype(jnp.bfloat16).T, class_in, preferred_element_type=jnp.float32
    ).astype(jnp.bfloat16)
    sent_grad = jnp.dot(
        placer.astype(jnp.bfloat16).T, class_scaled, preferred_element_type=jnp.float32
    ).astype(jnp.bfloat16)
    sent = jnp.stack(
        [sent_in.reshape(n_ex, per_class, width_part), sent_grad.reshape(n_ex, per_class, width_part)],
        axis=1,
    )
    sent = jnp.broadcast_to(sent[None], (n_class,) + sent.shape)
    sent = sent.reshape(n_class * n_ex, 2, per_class, width_part)
    got = lax.all_to_all(sent, LOCAL, 0, 0, tiled=True)
    rows = got.reshape(n_class, n_ex, 2, per_class, width_part).transpose(2, 0, 3, 1, 4)
    rows_in = rows[0].reshape(capacity, n_ex * width_part)
    rows_grad = rows[1].reshape(capacity, n_ex * width_part)

    gate_w, up_w, down_w = w_gate[0], w_up[0], w_down[0]
    partial, hidden, gate_delta, up_delta = row_math(got, gate_w, up_w, down_w, n_class, n_ex)
    down_grad = jnp.dot(hidden.T, rows_grad, preferred_element_type=jnp.float32).astype(
        jnp.bfloat16
    )
    gate_grad = jnp.dot(rows_in.T, gate_delta, preferred_element_type=jnp.float32).astype(
        jnp.bfloat16
    )
    up_grad = jnp.dot(rows_in.T, up_delta, preferred_element_type=jnp.float32).astype(jnp.bfloat16)
    back = lax.all_to_all(partial, LOCAL, 0, 0, tiled=True)
    back = back.reshape(n_class, n_ex * per_class, width_part)
    token_part = combine_tokens(back, column, n_z, tok)
    owned = lax.all_to_all(token_part, "z", 0, 0, tiled=True)
    input_grad = jnp.sum(owned, axis=0).astype(jnp.bfloat16)
    return (input_grad, gate_grad[None], up_grad[None], down_grad[None])


def solution(mesh):
    n_dp, n_ex = mesh.shape["dp"], mesh.shape["expert"]
    fine = Mesh(mesh.devices.reshape(n_dp // 4, 2, 2, 2, n_ex // 2), DP + EX)
    placed = (
        P(DP, EX),
        P(DP, None),
        P(DP, None),
        P(DP, EX),
        P(EX, None, DP),
        P(EX, None, DP),
        P(EX, DP, None),
    )
    return jax.shard_map(
        per_device,
        mesh=fine,
        in_specs=placed,
        out_specs=(
            P(DP, EX),
            P(EX, None, DP),
            P(EX, None, DP),
            P(EX, DP, None),
        ),
        check_vma=False,
    )
```

```python
import jax
import jax.numpy as jnp
from jax import lax
from jax.experimental import pallas as pl
from jax.experimental.pallas import tpu as pltpu
from jax.sharding import Mesh, PartitionSpec as P

MOST = 2
DP = ("z", "y_lo", "core")
EX = ("y_hi", "x")
CLASS = ("y_lo", "core")
LOCAL = CLASS + EX


def forward_part(rows_in, w_gate, w_up):
    gate_pre = jnp.dot(rows_in, w_gate, preferred_element_type=jnp.float32)
    up_pre = jnp.dot(rows_in, w_up, preferred_element_type=jnp.float32)
    gate_sig = jax.nn.sigmoid(gate_pre)
    activated = gate_pre * gate_sig
    hidden = (activated * up_pre).astype(jnp.bfloat16)
    return (gate_pre, up_pre, gate_sig, activated, hidden)


def pack_kernel(x_ref, cot_ref, comb_ref, rt_ref, o_ref, rows_ref):
    tok, width = x_ref.shape
    rows_ref[...] = jnp.zeros(rows_ref.shape, jnp.float32)
    rows_ref[0:tok, :] = x_ref[...].astype(jnp.float32)
    cot = cot_ref[...].astype(jnp.float32)
    lane = lax.broadcasted_iota(jnp.int32, (1, width), 1)
    route_row = jnp.zeros((1, width), jnp.float32)
    for k in range(2):
        for t in range(tok):
            a = k * tok + t
            row = (comb_ref[k, t] * cot[t : t + 1, :]).astype(jnp.bfloat16)
            rows_ref[tok + a : tok + a + 1, :] = row.astype(jnp.float32)
            route_row = jnp.where(lane == a, rt_ref[k, t].astype(jnp.float32), route_row)
    rows_ref[3 * tok : 3 * tok + 1, :] = route_row
    packed = rows_ref[...].astype(jnp.bfloat16)
    for z in range(o_ref.shape[0]):
        o_ref[z] = packed


def pack_block(inputs, cotangent, weights, routes, copies):
    tok, width = inputs.shape
    rows = 3 * tok + 1 + (-(3 * tok + 1)) % 16
    vmem = pl.BlockSpec(memory_space=pltpu.VMEM)
    smem = pl.BlockSpec(memory_space=pltpu.SMEM)
    return pl.pallas_call(
        pack_kernel,
        out_shape=jax.ShapeDtypeStruct((copies, rows, width), jnp.bfloat16),
        in_specs=[vmem, vmem, smem, smem],
        out_specs=vmem,
        scratch_shapes=[pltpu.VMEM((rows, width), jnp.float32)],
    )(inputs, cotangent, weights, routes)


def combine_kernel(back_ref, col_ref, o_ref, sum_ref):
    total = back_ref[0]
    for c in range(1, back_ref.shape[0]):
        total = total + back_ref[c]
    sum_ref[...] = total
    n_z, tok, width = o_ref.shape

    def block(zz, carry):
        for t in range(tok):
            acc = jnp.zeros((1, width), jnp.float32)
            for k in range(2):
                col = col_ref[zz * 2 * tok + k * tok + t]
                acc = acc + sum_ref[pl.ds(col, 1), :]
            o_ref[zz, pl.ds(t, 1), :] = acc
        return carry

    lax.fori_loop(0, n_z, block, 0, unroll=True)


def combine_tokens(back, column, n_z, tok):
    vmem = pl.BlockSpec(memory_space=pltpu.VMEM)
    smem = pl.BlockSpec(memory_space=pltpu.SMEM)
    return pl.pallas_call(
        combine_kernel,
        out_shape=jax.ShapeDtypeStruct((n_z, tok, back.shape[2]), jnp.float32),
        in_specs=[vmem, smem],
        out_specs=vmem,
        scratch_shapes=[pltpu.VMEM(back.shape[1:], jnp.float32)],
    )(back, column)


def per_device(inputs, routes, combine, cotangent, w_gate, w_up, w_down):
    tok = inputs.shape[0]
    width_part = inputs.shape[1]
    n_ex = lax.axis_size(EX)
    n_z = lax.axis_size("z")
    n_class = lax.axis_size(CLASS)
    per_class = n_z * MOST
    capacity = n_class * per_class
    slots_in_block = 2 * tok

    every = pack_block(inputs, cotangent, combine.T, routes.T, n_z)
    every = lax.all_to_all(every, "z", 0, 0, tiled=True)
    class_in = every[:, :tok, :].reshape(n_z * tok, width_part)
    class_scaled = every[:, tok : 3 * tok, :].reshape(n_z * slots_in_block, width_part)
    class_routes = every[:, 3 * tok, :slots_in_block].astype(jnp.int32)

    onehot = (class_routes[:, :, None] == jnp.arange(n_ex, dtype=jnp.int32)).astype(jnp.int32)
    before = jnp.cumsum(onehot, axis=1) - onehot
    rank = jnp.sum(before * onehot, axis=2)
    block_id = jnp.arange(n_z, dtype=jnp.int32)[:, None]
    column = (class_routes * per_class + block_id * MOST + rank).reshape(-1)
    placer = column[:, None] == jnp.arange(n_ex * per_class, dtype=jnp.int32)[None, :]
    placer_tok = jnp.any(placer.reshape(n_z, 2, tok, n_ex * per_class), axis=1)
    placer_tok = placer_tok.reshape(n_z * tok, n_ex * per_class)

    sent_in = jnp.dot(
        placer_tok.astype(jnp.bfloat16).T, class_in, preferred_element_type=jnp.float32
    ).astype(jnp.bfloat16)
    sent_grad = jnp.dot(
        placer.astype(jnp.bfloat16).T, class_scaled, preferred_element_type=jnp.float32
    ).astype(jnp.bfloat16)
    sent = jnp.stack(
        [sent_in.reshape(n_ex, per_class, width_part), sent_grad.reshape(n_ex, per_class, width_part)],
        axis=1,
    )
    sent = jnp.broadcast_to(sent[None], (n_class,) + sent.shape)
    sent = sent.reshape(n_class * n_ex, 2, per_class, width_part)
    got = lax.all_to_all(sent, LOCAL, 0, 0, tiled=True)
    got = got.reshape(n_class, n_ex, 2, per_class, width_part).transpose(2, 0, 3, 1, 4)
    rows_in = got[0].reshape(capacity, n_ex * width_part)
    rows_grad = got[1].reshape(capacity, n_ex * width_part)

    gate_w, up_w, down_w = w_gate[0], w_up[0], w_down[0]
    gate_pre, up_pre, gate_sig, activated, hidden = forward_part(rows_in, gate_w, up_w)
    hidden_delta = jnp.dot(rows_grad, down_w.T, preferred_element_type=jnp.float32)
    down_grad = jnp.dot(hidden.T, rows_grad, preferred_element_type=jnp.float32).astype(
        jnp.bfloat16
    )
    gate_delta = (hidden_delta * up_pre * gate_sig * (1.0 + gate_pre * (1.0 - gate_sig))).astype(
        jnp.bfloat16
    )
    up_delta = (hidden_delta * activated).astype(jnp.bfloat16)
    gate_grad = jnp.dot(rows_in.T, gate_delta, preferred_element_type=jnp.float32).astype(
        jnp.bfloat16
    )
    up_grad = jnp.dot(rows_in.T, up_delta, preferred_element_type=jnp.float32).astype(jnp.bfloat16)
    by_slice = (n_ex, width_part, gate_w.shape[1])
    from_gate = jnp.einsum(
        "csf,edf->cesd",
        gate_delta.reshape(n_class, per_class, -1),
        gate_w.reshape(by_slice),
        preferred_element_type=jnp.float32,
    )
    from_up = jnp.einsum(
        "csf,edf->cesd",
        up_delta.reshape(n_class, per_class, -1),
        up_w.reshape(by_slice),
        preferred_element_type=jnp.float32,
    )
    partial = (from_gate + from_up).reshape(n_class * n_ex, per_class, width_part)
    back = lax.all_to_all(partial, LOCAL, 0, 0, tiled=True)
    back = back.reshape(n_class, n_ex * per_class, width_part)
    token_part = combine_tokens(back, column, n_z, tok)
    owned = lax.all_to_all(token_part, "z", 0, 0, tiled=True)
    input_grad = jnp.sum(owned, axis=0).astype(jnp.bfloat16)
    return (input_grad, gate_grad[None], up_grad[None], down_grad[None])


def solution(mesh):
    n_dp, n_ex = mesh.shape["dp"], mesh.shape["expert"]
    fine = Mesh(mesh.devices.reshape(n_dp // 4, 2, 2, 2, n_ex // 2), DP + EX)
    placed = (
        P(DP, EX),
        P(DP, None),
        P(DP, None),
        P(DP, EX),
        P(EX, None, DP),
        P(EX, None, DP),
        P(EX, DP, None),
    )
    return jax.shard_map(
        per_device,
        mesh=fine,
        in_specs=placed,
        out_specs=(
            P(DP, EX),
            P(EX, None, DP),
            P(EX, None, DP),
            P(EX, DP, None),
        ),
        check_vma=False,
    )
```

```python
import jax
import jax.numpy as jnp
from jax import lax
from jax.experimental import pallas as pl
from jax.experimental.pallas import tpu as pltpu
from jax.sharding import Mesh, PartitionSpec as P

MOST = 2
DP = ("z", "y_lo", "core")
EX = ("y_hi", "x")
CLASS = ("y_lo", "core")
LOCAL = CLASS + EX


def forward_part(rows_in, w_gate, w_up):
    gate_pre = jnp.dot(rows_in, w_gate, preferred_element_type=jnp.float32)
    up_pre = jnp.dot(rows_in, w_up, preferred_element_type=jnp.float32)
    gate_sig = jax.nn.sigmoid(gate_pre)
    activated = gate_pre * gate_sig
    hidden = (activated * up_pre).astype(jnp.bfloat16)
    return (gate_pre, up_pre, gate_sig, activated, hidden)


def pack_kernel(x_ref, cot_ref, comb_ref, rt_ref, o_ref, rows_ref):
    tok, width = x_ref.shape
    rows_ref[...] = jnp.zeros(rows_ref.shape, jnp.float32)
    rows_ref[0:tok, :] = x_ref[...].astype(jnp.float32)
    cot = cot_ref[...].astype(jnp.float32)
    lane = lax.broadcasted_iota(jnp.int32, (1, width), 1)
    route_row = jnp.zeros((1, width), jnp.float32)
    for k in range(2):
        for t in range(tok):
            a = k * tok + t
            row = (comb_ref[k, t] * cot[t : t + 1, :]).astype(jnp.bfloat16)
            rows_ref[tok + a : tok + a + 1, :] = row.astype(jnp.float32)
            route_row = jnp.where(lane == a, rt_ref[k, t].astype(jnp.float32), route_row)
    rows_ref[3 * tok : 3 * tok + 1, :] = route_row
    packed = rows_ref[...].astype(jnp.bfloat16)
    for z in range(o_ref.shape[0]):
        o_ref[z] = packed


def pack_block(inputs, cotangent, weights, routes, copies):
    tok, width = inputs.shape
    rows = 3 * tok + 1 + (-(3 * tok + 1)) % 16
    vmem = pl.BlockSpec(memory_space=pltpu.VMEM)
    smem = pl.BlockSpec(memory_space=pltpu.SMEM)
    return pl.pallas_call(
        pack_kernel,
        out_shape=jax.ShapeDtypeStruct((copies, rows, width), jnp.bfloat16),
        in_specs=[vmem, vmem, smem, smem],
        out_specs=vmem,
        scratch_shapes=[pltpu.VMEM((rows, width), jnp.float32)],
    )(inputs, cotangent, weights, routes)


def combine_kernel(back_hbm, col_ref, o_ref, slab_ref, sum_ref, sems):
    copies = [
        pltpu.make_async_copy(back_hbm.at[c], slab_ref.at[c], sems.at[c])
        for c in range(back_hbm.shape[0])
    ]
    for copy in copies:
        copy.start()
    copies[0].wait()
    total = slab_ref[0]
    for c in range(1, len(copies)):
        copies[c].wait()
        total = total + slab_ref[c]
    sum_ref[...] = total
    n_z, tok, width = o_ref.shape

    def block(zz, carry):
        for t in range(tok):
            acc = jnp.zeros((1, width), jnp.float32)
            for k in range(2):
                col = col_ref[zz * 2 * tok + k * tok + t]
                acc = acc + sum_ref[pl.ds(col, 1), :]
            o_ref[zz, pl.ds(t, 1), :] = acc
        return carry

    lax.fori_loop(0, n_z, block, 0)


def combine_tokens(back, column, n_z, tok):
    vmem = pl.BlockSpec(memory_space=pltpu.VMEM)
    smem = pl.BlockSpec(memory_space=pltpu.SMEM)
    return pl.pallas_call(
        combine_kernel,
        out_shape=jax.ShapeDtypeStruct((n_z, tok, back.shape[2]), jnp.float32),
        in_specs=[pl.BlockSpec(memory_space=pl.ANY), smem],
        out_specs=vmem,
        scratch_shapes=[
            pltpu.VMEM(back.shape, jnp.float32),
            pltpu.VMEM(back.shape[1:], jnp.float32),
            pltpu.SemaphoreType.DMA((back.shape[0],)),
        ],
    )(back, column)


def per_device(inputs, routes, combine, cotangent, w_gate, w_up, w_down):
    tok = inputs.shape[0]
    width_part = inputs.shape[1]
    n_ex = lax.axis_size(EX)
    n_z = lax.axis_size("z")
    n_class = lax.axis_size(CLASS)
    per_class = n_z * MOST
    capacity = n_class * per_class
    slots_in_block = 2 * tok

    every = pack_block(inputs, cotangent, combine.T, routes.T, n_z)
    every = lax.all_to_all(every, "z", 0, 0, tiled=True)
    class_in = every[:, :tok, :].reshape(n_z * tok, width_part)
    class_scaled = every[:, tok : 3 * tok, :].reshape(n_z * slots_in_block, width_part)
    class_routes = every[:, 3 * tok, :slots_in_block].astype(jnp.int32)

    onehot = (class_routes[:, :, None] == jnp.arange(n_ex, dtype=jnp.int32)).astype(jnp.int32)
    before = jnp.cumsum(onehot, axis=1) - onehot
    rank = jnp.sum(before * onehot, axis=2)
    block_id = jnp.arange(n_z, dtype=jnp.int32)[:, None]
    column = (class_routes * per_class + block_id * MOST + rank).reshape(-1)
    placer = column[:, None] == jnp.arange(n_ex * per_class, dtype=jnp.int32)[None, :]
    placer_tok = jnp.any(placer.reshape(n_z, 2, tok, n_ex * per_class), axis=1)
    placer_tok = placer_tok.reshape(n_z * tok, n_ex * per_class)

    sent_in = jnp.dot(
        placer_tok.astype(jnp.bfloat16).T, class_in, preferred_element_type=jnp.float32
    ).astype(jnp.bfloat16)
    sent_grad = jnp.dot(
        placer.astype(jnp.bfloat16).T, class_scaled, preferred_element_type=jnp.float32
    ).astype(jnp.bfloat16)
    sent = jnp.stack(
        [sent_in.reshape(n_ex, per_class, width_part), sent_grad.reshape(n_ex, per_class, width_part)],
        axis=1,
    )
    sent = jnp.broadcast_to(sent[None], (n_class,) + sent.shape)
    sent = sent.reshape(n_class * n_ex, 2, per_class, width_part)
    got = lax.all_to_all(sent, LOCAL, 0, 0, tiled=True)
    got = got.reshape(n_class, n_ex, 2, per_class, width_part).transpose(2, 0, 3, 1, 4)
    rows_in = got[0].reshape(capacity, n_ex * width_part)
    rows_grad = got[1].reshape(capacity, n_ex * width_part)

    gate_w, up_w, down_w = w_gate[0], w_up[0], w_down[0]
    gate_pre, up_pre, gate_sig, activated, hidden = forward_part(rows_in, gate_w, up_w)
    hidden_delta = jnp.dot(rows_grad, down_w.T, preferred_element_type=jnp.float32)
    down_grad = jnp.dot(hidden.T, rows_grad, preferred_element_type=jnp.float32).astype(
        jnp.bfloat16
    )
    gate_delta = (hidden_delta * up_pre * gate_sig * (1.0 + gate_pre * (1.0 - gate_sig))).astype(
        jnp.bfloat16
    )
    up_delta = (hidden_delta * activated).astype(jnp.bfloat16)
    gate_grad = jnp.dot(rows_in.T, gate_delta, preferred_element_type=jnp.float32).astype(
        jnp.bfloat16
    )
    up_grad = jnp.dot(rows_in.T, up_delta, preferred_element_type=jnp.float32).astype(jnp.bfloat16)
    by_slice = (n_ex, width_part, gate_w.shape[1])
    from_gate = jnp.einsum(
        "csf,edf->cesd",
        gate_delta.reshape(n_class, per_class, -1),
        gate_w.reshape(by_slice),
        preferred_element_type=jnp.float32,
    )
    from_up = jnp.einsum(
        "csf,edf->cesd",
        up_delta.reshape(n_class, per_class, -1),
        up_w.reshape(by_slice),
        preferred_element_type=jnp.float32,
    )
    partial = (from_gate + from_up).reshape(n_class * n_ex, per_class, width_part)
    back = lax.all_to_all(partial, LOCAL, 0, 0, tiled=True)
    back = back.reshape(n_class, n_ex * per_class, width_part)
    token_part = combine_tokens(back, column, n_z, tok)
    owned = lax.all_to_all(token_part, "z", 0, 0, tiled=True)
    input_grad = jnp.sum(owned, axis=0).astype(jnp.bfloat16)
    return (input_grad, gate_grad[None], up_grad[None], down_grad[None])


def solution(mesh):
    n_dp, n_ex = mesh.shape["dp"], mesh.shape["expert"]
    fine = Mesh(mesh.devices.reshape(n_dp // 4, 2, 2, 2, n_ex // 2), DP + EX)
    placed = (
        P(DP, EX),
        P(DP, None),
        P(DP, None),
        P(DP, EX),
        P(EX, None, DP),
        P(EX, None, DP),
        P(EX, DP, None),
    )
    return jax.shard_map(
        per_device,
        mesh=fine,
        in_specs=placed,
        out_specs=(
            P(DP, EX),
            P(EX, None, DP),
            P(EX, None, DP),
            P(EX, DP, None),
        ),
        check_vma=False,
    )
```

```python
import jax
import jax.numpy as jnp
from jax import lax
from jax.experimental import pallas as pl
from jax.experimental.pallas import tpu as pltpu
from jax.sharding import Mesh, PartitionSpec as P

MOST = 2
DP = ("z", "y_lo", "core")
EX = ("y_hi", "x")
CLASS = ("y_lo", "core")
LOCAL = CLASS + EX


def forward_part(rows_in, w_gate, w_up):
    gate_pre = jnp.dot(rows_in, w_gate, preferred_element_type=jnp.float32)
    up_pre = jnp.dot(rows_in, w_up, preferred_element_type=jnp.float32)
    gate_sig = jax.nn.sigmoid(gate_pre)
    activated = gate_pre * gate_sig
    hidden = (activated * up_pre).astype(jnp.bfloat16)
    return (gate_pre, up_pre, gate_sig, activated, hidden)


def pack_kernel(x_ref, cot_ref, comb_ref, rt_ref, o_ref, rows_ref):
    tok, width = x_ref.shape
    rows_ref[...] = jnp.zeros(rows_ref.shape, jnp.float32)
    rows_ref[0:tok, :] = x_ref[...].astype(jnp.float32)
    cot = cot_ref[...].astype(jnp.float32)
    lane = lax.broadcasted_iota(jnp.int32, (1, width), 1)
    route_row = jnp.zeros((1, width), jnp.float32)
    for k in range(2):
        for t in range(tok):
            a = k * tok + t
            row = (comb_ref[k, t] * cot[t : t + 1, :]).astype(jnp.bfloat16)
            rows_ref[tok + a : tok + a + 1, :] = row.astype(jnp.float32)
            route_row = jnp.where(lane == a, rt_ref[k, t].astype(jnp.float32), route_row)
    rows_ref[3 * tok : 3 * tok + 1, :] = route_row
    packed = rows_ref[...].astype(jnp.bfloat16)
    for z in range(o_ref.shape[0]):
        o_ref[z] = packed


def pack_block(inputs, cotangent, weights, routes, copies):
    tok, width = inputs.shape
    rows = 3 * tok + 1 + (-(3 * tok + 1)) % 16
    vmem = pl.BlockSpec(memory_space=pltpu.VMEM)
    smem = pl.BlockSpec(memory_space=pltpu.SMEM)
    return pl.pallas_call(
        pack_kernel,
        out_shape=jax.ShapeDtypeStruct((copies, rows, width), jnp.bfloat16),
        in_specs=[vmem, vmem, smem, smem],
        out_specs=vmem,
        scratch_shapes=[pltpu.VMEM((rows, width), jnp.float32)],
    )(inputs, cotangent, weights, routes)


def combine_kernel(back_ref, col_ref, o_ref, sum_ref):
    total = back_ref[0]
    for c in range(1, back_ref.shape[0]):
        total = total + back_ref[c]
    sum_ref[...] = total
    n_z, tok, width = o_ref.shape

    def block(zz, carry):
        for t in range(tok):
            acc = jnp.zeros((1, width), jnp.float32)
            for k in range(2):
                col = col_ref[zz * 2 * tok + k * tok + t]
                acc = acc + sum_ref[pl.ds(col, 1), :]
            o_ref[zz, pl.ds(t, 1), :] = acc
        return carry

    lax.fori_loop(0, n_z, block, 0)


def combine_tokens(back, column, n_z, tok):
    vmem = pl.BlockSpec(memory_space=pltpu.VMEM)
    smem = pl.BlockSpec(memory_space=pltpu.SMEM)
    return pl.pallas_call(
        combine_kernel,
        out_shape=jax.ShapeDtypeStruct((n_z, tok, back.shape[2]), jnp.float32),
        in_specs=[vmem, smem],
        out_specs=vmem,
        scratch_shapes=[pltpu.VMEM(back.shape[1:], jnp.float32)],
    )(back, column)


def per_device(inputs, routes, combine, cotangent, w_gate, w_up, w_down):
    tok = inputs.shape[0]
    width_part = inputs.shape[1]
    n_ex = lax.axis_size(EX)
    n_z = lax.axis_size("z")
    n_class = lax.axis_size(CLASS)
    per_class = n_z * MOST
    capacity = n_class * per_class
    slots_in_block = 2 * tok

    every = pack_block(inputs, cotangent, combine.T, routes.T, n_z)
    every = lax.all_to_all(every, "z", 0, 0, tiled=True)
    class_in = every[:, :tok, :].reshape(n_z * tok, width_part)
    class_scaled = every[:, tok : 3 * tok, :].reshape(n_z * slots_in_block, width_part)
    class_routes = every[:, 3 * tok, :slots_in_block].astype(jnp.int32)

    onehot = (class_routes[:, :, None] == jnp.arange(n_ex, dtype=jnp.int32)).astype(jnp.int32)
    before = jnp.cumsum(onehot, axis=1) - onehot
    rank = jnp.sum(before * onehot, axis=2)
    block_id = jnp.arange(n_z, dtype=jnp.int32)[:, None]
    column = (class_routes * per_class + block_id * MOST + rank).reshape(-1)
    placer = column[:, None] == jnp.arange(n_ex * per_class, dtype=jnp.int32)[None, :]
    placer_tok = jnp.any(placer.reshape(n_z, 2, tok, n_ex * per_class), axis=1)
    placer_tok = placer_tok.reshape(n_z * tok, n_ex * per_class)

    sent_in = jnp.dot(
        placer_tok.astype(jnp.bfloat16).T, class_in, preferred_element_type=jnp.float32
    ).astype(jnp.bfloat16)
    sent_grad = jnp.dot(
        placer.astype(jnp.bfloat16).T, class_scaled, preferred_element_type=jnp.float32
    ).astype(jnp.bfloat16)
    sent = jnp.stack(
        [sent_in.reshape(n_ex, per_class, width_part), sent_grad.reshape(n_ex, per_class, width_part)],
        axis=1,
    )
    sent = jnp.broadcast_to(sent[None], (n_class,) + sent.shape)
    sent = sent.reshape(n_class * n_ex, 2, per_class, width_part)
    got_raw = lax.all_to_all(sent, LOCAL, 0, 0, tiled=True)
    got = got_raw.reshape(n_class, n_ex, 2, per_class, width_part).transpose(2, 0, 3, 1, 4)
    rows_in = got[0].reshape(capacity, n_ex * width_part)
    rows_grad = got[1].reshape(capacity, n_ex * width_part)

    gate_w, up_w, down_w = w_gate[0], w_up[0], w_down[0]
    by_slice = (n_ex, width_part, gate_w.shape[1])
    recv = got_raw.reshape(n_class, n_ex, 2, per_class, width_part)
    gate_pre = jnp.einsum(
        "cesd,edf->csf", recv[:, :, 0], gate_w.reshape(by_slice), preferred_element_type=jnp.float32
    ).reshape(capacity, -1)
    up_pre = jnp.einsum(
        "cesd,edf->csf", recv[:, :, 0], up_w.reshape(by_slice), preferred_element_type=jnp.float32
    ).reshape(capacity, -1)
    hidden_delta = jnp.einsum(
        "cesd,fed->csf",
        recv[:, :, 1],
        down_w.reshape(down_w.shape[0], n_ex, width_part),
        preferred_element_type=jnp.float32,
    ).reshape(capacity, -1)
    gate_sig = jax.nn.sigmoid(gate_pre)
    activated = gate_pre * gate_sig
    hidden = (activated * up_pre).astype(jnp.bfloat16)
    down_grad = jnp.dot(hidden.T, rows_grad, preferred_element_type=jnp.float32).astype(
        jnp.bfloat16
    )
    gate_delta = (hidden_delta * up_pre * gate_sig * (1.0 + gate_pre * (1.0 - gate_sig))).astype(
        jnp.bfloat16
    )
    up_delta = (hidden_delta * activated).astype(jnp.bfloat16)
    gate_grad = jnp.dot(rows_in.T, gate_delta, preferred_element_type=jnp.float32).astype(
        jnp.bfloat16
    )
    up_grad = jnp.dot(rows_in.T, up_delta, preferred_element_type=jnp.float32).astype(jnp.bfloat16)
    from_gate = jnp.einsum(
        "csf,edf->cesd",
        gate_delta.reshape(n_class, per_class, -1),
        gate_w.reshape(by_slice),
        preferred_element_type=jnp.float32,
    )
    from_up = jnp.einsum(
        "csf,edf->cesd",
        up_delta.reshape(n_class, per_class, -1),
        up_w.reshape(by_slice),
        preferred_element_type=jnp.float32,
    )
    partial = (from_gate + from_up).reshape(n_class * n_ex, per_class, width_part)
    back = lax.all_to_all(partial, LOCAL, 0, 0, tiled=True)
    back = back.reshape(n_class, n_ex * per_class, width_part)
    token_part = combine_tokens(back, column, n_z, tok)
    owned = lax.all_to_all(token_part, "z", 0, 0, tiled=True)
    input_grad = jnp.sum(owned, axis=0).astype(jnp.bfloat16)
    return (input_grad, gate_grad[None], up_grad[None], down_grad[None])


def solution(mesh):
    n_dp, n_ex = mesh.shape["dp"], mesh.shape["expert"]
    fine = Mesh(mesh.devices.reshape(n_dp // 4, 2, 2, 2, n_ex // 2), DP + EX)
    placed = (
        P(DP, EX),
        P(DP, None),
        P(DP, None),
        P(DP, EX),
        P(EX, None, DP),
        P(EX, None, DP),
        P(EX, DP, None),
    )
    return jax.shard_map(
        per_device,
        mesh=fine,
        in_specs=placed,
        out_specs=(
            P(DP, EX),
            P(EX, None, DP),
            P(EX, None, DP),
            P(EX, DP, None),
        ),
        check_vma=False,
    )
```
